32 devices in a mesh: seq: 8 (over z, y), fsdp: 4 (over x, core).
Axes of the slice: x: 2, y: 2, z: 4, core: 2. Of those that a mesh axis runs over, the one named last changes fastest.
Arguments:
- inputs: bfloat16 [12288, 1536], P(('seq', 'fsdp')), may hold values from -15 to 15
- layer_norm_gain: float32 [1536], replicated, may hold values from 0.25 to 1.75
- layer_norm_bias: float32 [1536], replicated, may hold values from -4 to 4
- w_in: bfloat16 [1536, 3072], P('fsdp'), may hold values from -0.15625 to 0.15625
- dw_kernel: float32 [32, 1536], replicated, may hold values from -1 to 1
- bn_gain: float32 [1536], replicated, may hold values from 0.25 to 1.75
- bn_bias: float32 [1536], replicated, may hold values from -4 to 4
- cotangent: bfloat16 [12288, 1536], P(('seq', 'fsdp')), may hold values from -6 to 6
Outputs:
- output: bfloat16 [12288, 1536], P(('seq', 'fsdp'))
- input_gradient: bfloat16 [12288, 1536], P(('seq', 'fsdp'))
- grad_w_in: float32 [1536, 3072], P('fsdp')
- grad_kernel: float32 [32, 1536], replicated
- grad_bn_gain: float32 [1536], replicated
- grad_bn_bias: float32 [1536], replicated
- layer_norm_gain_gradient: float32 [1536], replicated
- grad_ln_bias: float32 [1536], replicated
The draws below stay inside these ranges and needn't reach their ends.
All inputs are finite; a program needn't handle non-finite values.
Results may differ from the reference program's by a relative error of at most 0.012.
The reference program's roundings to bfloat16 on the way count: a program that leaves them out, or rounds other values in their place, can miss the bound.
Values may be sent and summed in bfloat16 or wider, within the bound.
No kernel may reach another device: no remote copies, remote signals or barrier semaphores. Data moves between devices by JAX's collectives and lax.ppermute only.
A program may use at most 128 MiB of HBM per device.

```python
import jax
import jax.numpy as jnp
from jax import lax

D = 1536
K = 32
TOKENS = 12288


def draw_inputs(key, part):
    noise_key = jax.random.fold_in(key, 11)
    direction_key = jax.random.fold_in(key, 12)
    direction = jnp.clip(jax.random.normal(direction_key, (D,), jnp.float32), -3.0, 3.0)
    position = jnp.arange(TOKENS, dtype=jnp.float32) / TOKENS
    noise = jnp.clip(jax.random.normal(noise_key, (TOKENS, D), jnp.float32), -6.0, 6.0)
    trend = 0.5 + 1.5 * position
    return (noise + trend[:, None] * direction[None, :]).astype(jnp.bfloat16)


def steps_of(stream_key, extent, split, smallest, high):
    loudness, own = 1.0, jax.random.fold_in(stream_key, 6)
    for dim, shards_of in split:
        draws = jnp.exp(jax.random.uniform(jax.random.fold_in(own, dim), (shards_of,), jnp.float32, smallest / len(split), high / len(split)))
        loudness = loudness * jnp.repeat(draws, extent[dim] // shards_of).reshape([-1 if axis == dim else 1 for axis in range(len(extent))])
    return loudness


def scatter_about(stream_key, extent, scale, reach, shards=(), kind=jnp.bfloat16):
    entries = jax.random.normal(stream_key, extent, jnp.float32) * scale
    if len(shards) > 0:
        entries = steps_of(stream_key, extent, shards, -0.22, 0.18) * entries
    return jnp.clip(entries, min=-reach, max=reach).astype(kind)


def setup_inputs(seed: int = 0) -> dict:
    key_of = jax.random.split(jax.random.key(seed), 9)
    return {
        "inputs": draw_inputs(jax.random.fold_in(key_of[8], 71), 0),
        "layer_norm_gain": jnp.clip(1.0 + 0.15 * jax.random.normal(key_of[1], (D,), jnp.float32), 0.25, 1.75),
        "layer_norm_bias": scatter_about(key_of[2], (D,), 0.4, 4.0, (), jnp.float32),
        "w_in": scatter_about(key_of[3], (D, 2 * D), D ** -0.5, 0.15625, ((0, 4),)),
        "dw_kernel": scatter_about(key_of[4], (K, D), K ** -0.5, 1.0, (), jnp.float32),
        "bn_gain": jnp.clip(1.0 + 0.15 * jax.random.normal(key_of[5], (D,), jnp.float32), 0.25, 1.75),
        "bn_bias": scatter_about(key_of[6], (D,), 0.5, 4.0, (), jnp.float32),
        "cotangent": scatter_about(key_of[7], (TOKENS, D), 1.0, 6.0, ((0, 32),)),
    }


epsilon = 1e-05

def reference(inputs, layer_norm_gain, layer_norm_bias, w_in, dw_kernel, bn_gain, bn_bias, cotangent):
    frames = inputs.astype(jnp.float32)
    row_mean = lax.optimization_barrier(jnp.mean(frames, axis=-1, keepdims=True))
    centered_rows = frames - row_mean
    row_inverse_deviation = lax.rsqrt(lax.optimization_barrier(jnp.mean(centered_rows * centered_rows, axis=-1, keepdims=True)) + epsilon)
    standardized_input = centered_rows * row_inverse_deviation
    normalized_rows = (standardized_input * layer_norm_gain + layer_norm_bias).astype(jnp.bfloat16)
    hidden = jnp.dot(normalized_rows, w_in, preferred_element_type=jnp.float32)
    value_part = hidden[:, :D]
    gate_sig = jax.nn.sigmoid(hidden[:, D:])
    glu = (value_part * gate_sig).astype(jnp.bfloat16)
    padded_glu = jnp.pad(glu.astype(jnp.float32), ((K - 1, 0), (0, 0)))
    conv_out = jnp.zeros((TOKENS, D), jnp.float32)
    for offset in range(K):
        conv_out = conv_out + dw_kernel[offset] * padded_glu[K - 1 - offset:K - 1 - offset + TOKENS]
    chan_mean = lax.optimization_barrier(jnp.mean(conv_out, axis=0))
    conv_centred = conv_out - chan_mean
    bn_rstd = lax.rsqrt(lax.optimization_barrier(jnp.mean(conv_centred * conv_centred, axis=0)) + epsilon)
    chat = conv_centred * bn_rstd
    z_value = chat * bn_gain + bn_bias
    z_sig = jax.nn.sigmoid(z_value)
    output = (z_value * z_sig).astype(jnp.bfloat16)
    grad_z = cotangent.astype(jnp.float32) * z_sig * (1.0 + z_value * (1.0 - z_sig))
    grad_bn_bias = lax.optimization_barrier(jnp.sum(grad_z, axis=0))
    grad_bn_gain = lax.optimization_barrier(jnp.sum(grad_z * chat, axis=0))
    grad_conv = bn_gain * bn_rstd * (grad_z - grad_bn_bias / TOKENS - chat * grad_bn_gain / TOKENS)
    padded_grad = jnp.pad(grad_conv, ((0, K - 1), (0, 0)))
    grad_glu = jnp.zeros((TOKENS, D), jnp.float32)
    kernel_rows = []
    for offset in range(K):
        grad_glu = grad_glu + dw_kernel[offset] * padded_grad[offset:offset + TOKENS]
        kernel_rows.append(lax.optimization_barrier(jnp.sum(grad_conv * padded_glu[K - 1 - offset:K - 1 - offset + TOKENS], axis=0)))
    grad_kernel = jnp.stack(kernel_rows, axis=0)
    grad_value = grad_glu * gate_sig
    grad_gate = grad_glu * value_part * gate_sig * (1.0 - gate_sig)
    grad_hidden = jnp.concatenate([grad_value, grad_gate], axis=1).astype(jnp.bfloat16)
    normalized_gradient = lax.dot_general(grad_hidden, w_in, (((1,), (1,)), ((), ())), preferred_element_type=jnp.float32)
    grad_w_in = lax.dot_general(normalized_rows, grad_hidden, (((0,), (0,)), ((), ())), preferred_element_type=jnp.float32)
    layer_norm_gain_gradient = lax.optimization_barrier(jnp.sum(normalized_gradient * standardized_input, axis=0))
    grad_ln_bias = lax.optimization_barrier(jnp.sum(normalized_gradient, axis=0))
    rescaled_rows = normalized_gradient * layer_norm_gain
    input_gradient = row_inverse_deviation * (rescaled_rows - lax.optimization_barrier(jnp.mean(rescaled_rows, axis=-1, keepdims=True)) - standardized_input * lax.optimization_barrier(jnp.mean(rescaled_rows * standardized_input, axis=-1, keepdims=True)))
    return (output, input_gradient.astype(jnp.bfloat16), grad_w_in, grad_kernel, grad_bn_gain, grad_bn_bias, layer_norm_gain_gradient, grad_ln_bias)
```

```python
import jax
import jax.numpy as jnp
from jax import lax
from jax.sharding import PartitionSpec as P

epsilon = 1e-05


def from_behind(block, axis, distance):
    devices = range(lax.axis_size(axis))
    route = [(i - distance, i) for i in devices if i - distance in devices]
    return lax.ppermute(block, axis, route)


def tree_sum(tree, axis):
    count = lax.axis_size(axis)
    if count & (count - 1):
        return lax.psum(tree, axis)
    stride = 1
    while stride < count:
        route = [(i, i ^ stride) for i in range(count)]
        tree = jax.tree.map(lambda x: x + lax.ppermute(x, axis, route), tree)
        stride *= 2
    return tree


def on_device(
    inputs, layer_norm_gain, layer_norm_bias, w_in, dw_kernel, bn_gain, bn_bias, cotangent
):
    tok_rows = inputs.shape[0]
    features = inputs.shape[1]
    kernel_len = dw_kernel.shape[0]
    all_frames = tok_rows * lax.axis_size("seq") * lax.axis_size("fsdp")
    frames = inputs.astype(jnp.float32)
    row_mean = jnp.mean(frames, axis=-1, keepdims=True)
    centered_rows = frames - row_mean
    row_inverse_deviation = lax.rsqrt(
        jnp.mean(centered_rows * centered_rows, axis=-1, keepdims=True) + epsilon
    )
    standardized_input = centered_rows * row_inverse_deviation
    normalized_rows = (standardized_input * layer_norm_gain + layer_norm_bias).astype(jnp.bfloat16)
    full_weight = lax.all_gather(w_in, "fsdp", axis=0, tiled=True)
    hidden = jnp.dot(normalized_rows, full_weight, preferred_element_type=jnp.float32)
    value_part = hidden[:, :features]
    gate_sig = jax.nn.sigmoid(hidden[:, features:])
    glu = (value_part * gate_sig).astype(jnp.bfloat16)
    past_rim = from_behind(glu[tok_rows - (kernel_len - 1) :], ("seq", "fsdp"), 1)
    padded_glu = jnp.concatenate([past_rim, glu], axis=0).astype(jnp.float32)
    conv_out = jnp.zeros((tok_rows, features), jnp.float32)
    for offset in range(kernel_len):
        conv_out = (
            conv_out
            + dw_kernel[offset]
            * padded_glu[kernel_len - 1 - offset : kernel_len - 1 - offset + tok_rows]
        )
    chan_mean = tree_sum(jnp.sum(conv_out, axis=0), ("seq", "fsdp")) / all_frames
    conv_centred = conv_out - chan_mean
    chan_var = tree_sum(jnp.sum(conv_centred * conv_centred, axis=0), ("seq", "fsdp")) / all_frames
    bn_rstd = lax.rsqrt(chan_var + epsilon)
    chat = conv_centred * bn_rstd
    z_value = chat * bn_gain + bn_bias
    z_sig = jax.nn.sigmoid(z_value)
    output = (z_value * z_sig).astype(jnp.bfloat16)
    grad_z = cotangent.astype(jnp.float32) * z_sig * (1.0 + z_value * (1.0 - z_sig))
    grad_bn_bias, grad_bn_gain = tree_sum(
        (jnp.sum(grad_z, axis=0), jnp.sum(grad_z * chat, axis=0)), ("seq", "fsdp")
    )
    grad_conv = (
        bn_gain * bn_rstd * (grad_z - grad_bn_bias / all_frames - chat * grad_bn_gain / all_frames)
    )
    future_rim = from_behind(grad_conv[: kernel_len - 1], ("seq", "fsdp"), -1)
    padded_grad = jnp.concatenate([grad_conv, future_rim], axis=0)
    grad_glu = jnp.zeros((tok_rows, features), jnp.float32)
    kernel_rows = []
    for offset in range(kernel_len):
        grad_glu = grad_glu + dw_kernel[offset] * padded_grad[offset : offset + tok_rows]
        kernel_rows.append(
            jnp.sum(
                grad_conv
                * padded_glu[kernel_len - 1 - offset : kernel_len - 1 - offset + tok_rows],
                axis=0,
            )
        )
    kernel_portion = jnp.stack(kernel_rows, axis=0)
    grad_value = grad_glu * gate_sig
    grad_gate = grad_glu * value_part * gate_sig * (1.0 - gate_sig)
    grad_hidden = jnp.concatenate([grad_value, grad_gate], axis=1).astype(jnp.bfloat16)
    normalized_gradient = lax.dot_general(
        grad_hidden, full_weight, (((1,), (1,)), ((), ())), preferred_element_type=jnp.float32
    )
    grad_kernel, layer_norm_gain_gradient, grad_ln_bias = tree_sum(
        (
            kernel_portion,
            jnp.sum(normalized_gradient * standardized_input, axis=0),
            jnp.sum(normalized_gradient, axis=0),
        ),
        ("seq", "fsdp"),
    )
    rescaled_rows = normalized_gradient * layer_norm_gain
    input_gradient = row_inverse_deviation * (
        rescaled_rows
        - jnp.mean(rescaled_rows, axis=-1, keepdims=True)
        - standardized_input * jnp.mean(rescaled_rows * standardized_input, axis=-1, keepdims=True)
    )
    row_share = lax.psum_scatter(
        lax.dot_general(
            normalized_rows,
            grad_hidden,
            (((0,), (0,)), ((), ())),
            preferred_element_type=jnp.float32,
        ),
        "fsdp",
        scatter_dimension=0,
        tiled=True,
    )
    grad_w_in = lax.psum(row_share, "seq")
    return (
        output,
        input_gradient.astype(jnp.bfloat16),
        grad_w_in,
        grad_kernel,
        grad_bn_gain,
        grad_bn_bias,
        layer_norm_gain_gradient,
        grad_ln_bias,
    )


def solution(mesh):
    placed = (
        P(("seq", "fsdp"), None),
        P(),
        P(),
        P("fsdp", None),
        P(),
        P(),
        P(),
        P(("seq", "fsdp"), None),
    )
    return jax.shard_map(
        on_device,
        mesh=mesh,
        in_specs=placed,
        out_specs=(
            P(("seq", "fsdp"), None),
            P(("seq", "fsdp"), None),
            P("fsdp", None),
            P(),
            P(),
            P(),
            P(),
            P(),
        ),
        check_vma=False,
    )
```

```python
import jax
import jax.numpy as jnp
from jax import lax
from jax.sharding import PartitionSpec as P

epsilon = 1e-05


def from_behind(block, axis, distance):
    devices = range(lax.axis_size(axis))
    route = [(i - distance, i) for i in devices if i - distance in devices]
    return lax.ppermute(block, axis, route)


def tree_sum(tree, axis):
    count = lax.axis_size(axis)
    if count & (count - 1):
        return lax.psum(tree, axis)
    stride = 1
    while stride < count:
        route = [(i, i ^ stride) for i in range(count)]
        tree = jax.tree.map(lambda x: x + lax.ppermute(x, axis, route), tree)
        stride *= 2
    return tree


def on_device(
    inputs, layer_norm_gain, layer_norm_bias, w_in, dw_kernel, bn_gain, bn_bias, cotangent
):
    tok_rows = inputs.shape[0]
    features = inputs.shape[1]
    kernel_len = dw_kernel.shape[0]
    all_frames = tok_rows * lax.axis_size("seq") * lax.axis_size("fsdp")
    frames = inputs.astype(jnp.float32)
    row_mean = jnp.mean(frames, axis=-1, keepdims=True)
    centered_rows = frames - row_mean
    row_inverse_deviation = lax.rsqrt(
        jnp.mean(centered_rows * centered_rows, axis=-1, keepdims=True) + epsilon
    )
    standardized_input = centered_rows * row_inverse_deviation
    normalized_rows = (standardized_input * layer_norm_gain + layer_norm_bias).astype(jnp.bfloat16)
    full_weight = lax.all_gather(w_in, "fsdp", axis=0, tiled=True)
    group_rows = lax.all_gather(normalized_rows, "fsdp", axis=0, tiled=True)
    hidden = jnp.dot(normalized_rows, full_weight, preferred_element_type=jnp.float32)
    value_part = hidden[:, :features]
    gate_sig = jax.nn.sigmoid(hidden[:, features:])
    glu = (value_part * gate_sig).astype(jnp.bfloat16)
    past_rim = from_behind(glu[tok_rows - (kernel_len - 1) :], ("seq", "fsdp"), 1)
    padded_glu = jnp.concatenate([past_rim, glu], axis=0).astype(jnp.float32)
    conv_out = jnp.zeros((tok_rows, features), jnp.float32)
    for offset in range(kernel_len):
        conv_out = (
            conv_out
            + dw_kernel[offset]
            * padded_glu[kernel_len - 1 - offset : kernel_len - 1 - offset + tok_rows]
        )
    chan_mean = tree_sum(jnp.sum(conv_out, axis=0), ("seq", "fsdp")) / all_frames
    conv_centred = conv_out - chan_mean
    chan_var = tree_sum(jnp.sum(conv_centred * conv_centred, axis=0), ("seq", "fsdp")) / all_frames
    bn_rstd = lax.rsqrt(chan_var + epsilon)
    chat = conv_centred * bn_rstd
    z_value = chat * bn_gain + bn_bias
    z_sig = jax.nn.sigmoid(z_value)
    output = (z_value * z_sig).astype(jnp.bfloat16)
    grad_z = cotangent.astype(jnp.float32) * z_sig * (1.0 + z_value * (1.0 - z_sig))
    grad_bn_bias, grad_bn_gain = tree_sum(
        (jnp.sum(grad_z, axis=0), jnp.sum(grad_z * chat, axis=0)), ("seq", "fsdp")
    )
    grad_conv = (
        bn_gain * bn_rstd * (grad_z - grad_bn_bias / all_frames - chat * grad_bn_gain / all_frames)
    )
    future_rim = from_behind(grad_conv[: kernel_len - 1], ("seq", "fsdp"), -1)
    padded_grad = jnp.concatenate([grad_conv, future_rim], axis=0)
    grad_glu = jnp.zeros((tok_rows, features), jnp.float32)
    kernel_rows = []
    for offset in range(kernel_len):
        grad_glu = grad_glu + dw_kernel[offset] * padded_grad[offset : offset + tok_rows]
        kernel_rows.append(
            jnp.sum(
                grad_conv
                * padded_glu[kernel_len - 1 - offset : kernel_len - 1 - offset + tok_rows],
                axis=0,
            )
        )
    kernel_portion = jnp.stack(kernel_rows, axis=0)
    grad_value = grad_glu * gate_sig
    grad_gate = grad_glu * value_part * gate_sig * (1.0 - gate_sig)
    grad_hidden = jnp.concatenate([grad_value, grad_gate], axis=1).astype(jnp.bfloat16)
    normalized_gradient = lax.dot_general(
        grad_hidden, full_weight, (((1,), (1,)), ((), ())), preferred_element_type=jnp.float32
    )
    grad_kernel, layer_norm_gain_gradient, grad_ln_bias = tree_sum(
        (
            kernel_portion,
            jnp.sum(normalized_gradient * standardized_input, axis=0),
            jnp.sum(normalized_gradient, axis=0),
        ),
        ("seq", "fsdp"),
    )
    rescaled_rows = normalized_gradient * layer_norm_gain
    input_gradient = row_inverse_deviation * (
        rescaled_rows
        - jnp.mean(rescaled_rows, axis=-1, keepdims=True)
        - standardized_input * jnp.mean(rescaled_rows * standardized_input, axis=-1, keepdims=True)
    )
    feature_rows = w_in.shape[0]
    own_columns = lax.dynamic_slice_in_dim(
        group_rows, lax.axis_index("fsdp") * feature_rows, feature_rows, axis=1
    )
    group_grad = lax.all_gather(grad_hidden, "fsdp", axis=0, tiled=True)
    row_share = lax.dot_general(
        own_columns, group_grad, (((0,), (0,)), ((), ())), preferred_element_type=jnp.float32
    )
    grad_w_in = lax.psum(row_share, "seq")
    return (
        output,
        input_gradient.astype(jnp.bfloat16),
        grad_w_in,
        grad_kernel,
        grad_bn_gain,
        grad_bn_bias,
        layer_norm_gain_gradient,
        grad_ln_bias,
    )


def solution(mesh):
    placed = (
        P(("seq", "fsdp"), None),
        P(),
        P(),
        P("fsdp", None),
        P(),
        P(),
        P(),
        P(("seq", "fsdp"), None),
    )
    return jax.shard_map(
        on_device,
        mesh=mesh,
        in_specs=placed,
        out_specs=(
            P(("seq", "fsdp"), None),
            P(("seq", "fsdp"), None),
            P("fsdp", None),
            P(),
            P(),
            P(),
            P(),
            P(),
        ),
        check_vma=False,
    )
```

```python
import jax
import jax.numpy as jnp
from jax import lax
from jax.sharding import PartitionSpec as P

epsilon = 1e-05


def from_behind(block, axis, distance):
    devices = range(lax.axis_size(axis))
    route = [(i - distance, i) for i in devices if i - distance in devices]
    return lax.ppermute(block, axis, route)


def tree_sum(tree, axis):
    count = lax.axis_size(axis)
    if count & (count - 1):
        return lax.psum(tree, axis)
    leaves, treedef = jax.tree.flatten(tree)
    width = leaves[0].shape[-1]
    packed = jnp.concatenate([leaf.reshape(-1, width) for leaf in leaves], axis=0)
    stride = 1
    while stride < count:
        route = [(i, i ^ stride) for i in range(count)]
        packed = packed + lax.ppermute(packed, axis, route)
        stride *= 2
    out, start = [], 0
    for leaf in leaves:
        rows = leaf.size // width
        out.append(packed[start : start + rows].reshape(leaf.shape))
        start += rows
    return jax.tree.unflatten(treedef, out)


def group_shards(block, axis):
    far = lax.ppermute(block, axis, [(i, i ^ 2) for i in range(4)])
    near = lax.ppermute(
        jnp.concatenate([block, far], axis=0), axis, [(i, i ^ 1) for i in range(4)]
    )
    return jnp.concatenate([block, far, near], axis=0)


def gather_rows(block, axis):
    count = lax.axis_size(axis)
    if count != 4:
        return lax.all_gather(block, axis, axis=0, tiled=True)
    rows = block.shape[0]
    me = lax.axis_index(axis)
    shards = group_shards(block, axis)
    whole = jnp.zeros((count * rows,) + block.shape[1:], block.dtype)
    for slot, owner in enumerate((me, me ^ 2, me ^ 1, me ^ 3)):
        whole = lax.dynamic_update_slice_in_dim(
            whole, shards[slot * rows : (slot + 1) * rows], owner * rows, axis=0
        )
    return whole


def gather_own_columns(rows_block, axis, width):
    me = lax.axis_index(axis)
    frames = rows_block.shape[0]

    def cols(owner):
        return lax.dynamic_slice_in_dim(rows_block, owner * width, width, axis=1)

    if lax.axis_size(axis) != 4:
        return lax.dynamic_slice_in_dim(
            lax.all_gather(rows_block, axis, axis=0, tiled=True), me * width, width, axis=1
        )
    far = lax.ppermute(
        jnp.concatenate([cols(me ^ 2), cols(me ^ 3)], axis=0), axis, [(i, i ^ 2) for i in range(4)]
    )
    near = lax.ppermute(
        jnp.concatenate([cols(me ^ 1), far[frames:]], axis=0), axis, [(i, i ^ 1) for i in range(4)]
    )
    return jnp.concatenate([cols(me), far[:frames], near], axis=0)


def gather_frames(block, axis):
    if lax.axis_size(axis) != 4:
        return lax.all_gather(block, axis, axis=0, tiled=True)
    return group_shards(block, axis)


def on_device(
    inputs, layer_norm_gain, layer_norm_bias, w_in, dw_kernel, bn_gain, bn_bias, cotangent
):
    tok_rows = inputs.shape[0]
    features = inputs.shape[1]
    kernel_len = dw_kernel.shape[0]
    all_frames = tok_rows * lax.axis_size("seq") * lax.axis_size("fsdp")
    frames = inputs.astype(jnp.float32)
    row_mean = jnp.mean(frames, axis=-1, keepdims=True)
    centered_rows = frames - row_mean
    row_inverse_deviation = lax.rsqrt(
        jnp.mean(centered_rows * centered_rows, axis=-1, keepdims=True) + epsilon
    )
    standardized_input = centered_rows * row_inverse_deviation
    normalized_rows = (standardized_input * layer_norm_gain + layer_norm_bias).astype(jnp.bfloat16)
    full_weight = gather_rows(w_in, "fsdp")
    hidden = jnp.dot(normalized_rows, full_weight, preferred_element_type=jnp.float32)
    value_part = hidden[:, :features]
    gate_sig = jax.nn.sigmoid(hidden[:, features:])
    glu = (value_part * gate_sig).astype(jnp.bfloat16)
    past_rim = from_behind(glu[tok_rows - (kernel_len - 1) :], ("seq", "fsdp"), 1)
    padded_glu = jnp.concatenate([past_rim, glu], axis=0).astype(jnp.float32)
    conv_out = jnp.zeros((tok_rows, features), jnp.float32)
    for offset in range(kernel_len):
        conv_out = (
            conv_out
            + dw_kernel[offset]
            * padded_glu[kernel_len - 1 - offset : kernel_len - 1 - offset + tok_rows]
        )
    chan_mean = tree_sum(jnp.sum(conv_out, axis=0), ("seq", "fsdp")) / all_frames
    conv_centred = conv_out - chan_mean
    chan_var = tree_sum(jnp.sum(conv_centred * conv_centred, axis=0), ("seq", "fsdp")) / all_frames
    bn_rstd = lax.rsqrt(chan_var + epsilon)
    chat = conv_centred * bn_rstd
    z_value = chat * bn_gain + bn_bias
    z_sig = jax.nn.sigmoid(z_value)
    output = (z_value * z_sig).astype(jnp.bfloat16)
    grad_z = cotangent.astype(jnp.float32) * z_sig * (1.0 + z_value * (1.0 - z_sig))
    grad_bn_bias, grad_bn_gain = tree_sum(
        (jnp.sum(grad_z, axis=0), jnp.sum(grad_z * chat, axis=0)), ("seq", "fsdp")
    )
    grad_conv = (
        bn_gain * bn_rstd * (grad_z - grad_bn_bias / all_frames - chat * grad_bn_gain / all_frames)
    )
    future_rim = from_behind(grad_conv[: kernel_len - 1], ("seq", "fsdp"), -1)
    padded_grad = jnp.concatenate([grad_conv, future_rim], axis=0)
    grad_glu = jnp.zeros((tok_rows, features), jnp.float32)
    kernel_rows = []
    for offset in range(kernel_len):
        grad_glu = grad_glu + dw_kernel[offset] * padded_grad[offset : offset + tok_rows]
        kernel_rows.append(
            jnp.sum(
                grad_conv
                * padded_glu[kernel_len - 1 - offset : kernel_len - 1 - offset + tok_rows],
                axis=0,
            )
        )
    kernel_portion = jnp.stack(kernel_rows, axis=0)
    grad_value = grad_glu * gate_sig
    grad_gate = grad_glu * value_part * gate_sig * (1.0 - gate_sig)
    grad_hidden = jnp.concatenate([grad_value, grad_gate], axis=1).astype(jnp.bfloat16)
    normalized_gradient = lax.dot_general(
        grad_hidden, full_weight, (((1,), (1,)), ((), ())), preferred_element_type=jnp.float32
    )
    grad_kernel, layer_norm_gain_gradient, grad_ln_bias = tree_sum(
        (
            kernel_portion,
            jnp.sum(normalized_gradient * standardized_input, axis=0),
            jnp.sum(normalized_gradient, axis=0),
        ),
        ("seq", "fsdp"),
    )
    rescaled_rows = normalized_gradient * layer_norm_gain
    input_gradient = row_inverse_deviation * (
        rescaled_rows
        - jnp.mean(rescaled_rows, axis=-1, keepdims=True)
        - standardized_input * jnp.mean(rescaled_rows * standardized_input, axis=-1, keepdims=True)
    )
    feature_rows = w_in.shape[0]
    group_rows = gather_own_columns(normalized_rows, "fsdp", feature_rows)
    group_grad = gather_frames(grad_hidden, "fsdp")
    row_share = lax.dot_general(
        group_rows, group_grad, (((0,), (0,)), ((), ())), preferred_element_type=jnp.float32
    )
    grad_w_in = lax.psum(row_share, "seq")
    return (
        output,
        input_gradient.astype(jnp.bfloat16),
        grad_w_in,
        grad_kernel,
        grad_bn_gain,
        grad_bn_bias,
        layer_norm_gain_gradient,
        grad_ln_bias,
    )


def solution(mesh):
    placed = (
        P(("seq", "fsdp"), None),
        P(),
        P(),
        P("fsdp", None),
        P(),
        P(),
        P(),
        P(("seq", "fsdp"), None),
    )
    return jax.shard_map(
        on_device,
        mesh=mesh,
        in_specs=placed,
        out_specs=(
            P(("seq", "fsdp"), None),
            P(("seq", "fsdp"), None),
            P("fsdp", None),
            P(),
            P(),
            P(),
            P(),
            P(),
        ),
        check_vma=False,
    )
```

```python
import jax
import jax.numpy as jnp
from jax import lax
from jax.sharding import PartitionSpec as P

epsilon = 1e-05


def from_behind(block, axis, distance):
    devices = range(lax.axis_size(axis))
    route = [(i - distance, i) for i in devices if i - distance in devices]
    return lax.ppermute(block, axis, route)


def tree_sum(tree, axis):
    count = lax.axis_size(axis)
    if count & (count - 1):
        return lax.psum(tree, axis)
    leaves, treedef = jax.tree.flatten(tree)
    width = leaves[0].shape[-1]
    packed = jnp.concatenate([leaf.reshape(-1, width) for leaf in leaves], axis=0)
    stride = 1
    while stride < count:
        route = [(i, i ^ stride) for i in range(count)]
        packed = packed + lax.ppermute(packed, axis, route)
        stride *= 2
    out, start = [], 0
    for leaf in leaves:
        rows = leaf.size // width
        out.append(packed[start : start + rows].reshape(leaf.shape))
        start += rows
    return jax.tree.unflatten(treedef, out)


def group_shards(block, axis):
    far = lax.ppermute(block, axis, [(i, i ^ 2) for i in range(4)])
    near = lax.ppermute(
        jnp.concatenate([block, far], axis=0), axis, [(i, i ^ 1) for i in range(4)]
    )
    return jnp.concatenate([block, far, near], axis=0)


def gather_rows(block, axis):
    count = lax.axis_size(axis)
    if count != 4:
        return lax.all_gather(block, axis, axis=0, tiled=True)
    rows = block.shape[0]
    me = lax.axis_index(axis)
    shards = group_shards(block, axis)
    whole = jnp.zeros((count * rows,) + block.shape[1:], block.dtype)
    for slot, owner in enumerate((me, me ^ 2, me ^ 1, me ^ 3)):
        whole = lax.dynamic_update_slice_in_dim(
            whole, shards[slot * rows : (slot + 1) * rows], owner * rows, axis=0
        )
    return whole


def gather_own_columns(rows_block, axis, width):
    me = lax.axis_index(axis)
    frames = rows_block.shape[0]

    def cols(owner):
        return lax.dynamic_slice_in_dim(rows_block, owner * width, width, axis=1)

    if lax.axis_size(axis) != 4:
        return lax.dynamic_slice_in_dim(
            lax.all_gather(rows_block, axis, axis=0, tiled=True), me * width, width, axis=1
        )
    far = lax.ppermute(
        jnp.concatenate([cols(me ^ 2), cols(me ^ 3)], axis=0), axis, [(i, i ^ 2) for i in range(4)]
    )
    near = lax.ppermute(
        jnp.concatenate([cols(me ^ 1), far[frames:]], axis=0), axis, [(i, i ^ 1) for i in range(4)]
    )
    return jnp.concatenate([cols(me), far[:frames], near], axis=0)


def gather_frames(block, axis):
    if lax.axis_size(axis) != 4:
        return lax.all_gather(block, axis, axis=0, tiled=True)
    return group_shards(block, axis)


def on_device(
    inputs, layer_norm_gain, layer_norm_bias, w_in, dw_kernel, bn_gain, bn_bias, cotangent
):
    tok_rows = inputs.shape[0]
    features = inputs.shape[1]
    kernel_len = dw_kernel.shape[0]
    all_frames = tok_rows * lax.axis_size("seq") * lax.axis_size("fsdp")
    frames = inputs.astype(jnp.float32)
    row_mean = jnp.mean(frames, axis=-1, keepdims=True)
    centered_rows = frames - row_mean
    row_inverse_deviation = lax.rsqrt(
        jnp.mean(centered_rows * centered_rows, axis=-1, keepdims=True) + epsilon
    )
    standardized_input = centered_rows * row_inverse_deviation
    normalized_rows = (standardized_input * layer_norm_gain + layer_norm_bias).astype(jnp.bfloat16)
    full_weight = gather_rows(w_in, "fsdp")
    hidden = jnp.dot(normalized_rows, full_weight, preferred_element_type=jnp.float32)
    value_part = hidden[:, :features]
    gate_sig = jax.nn.sigmoid(hidden[:, features:])
    glu = (value_part * gate_sig).astype(jnp.bfloat16)
    past_rim = from_behind(glu[tok_rows - (kernel_len - 1) :], ("seq", "fsdp"), 1)
    padded_glu = jnp.concatenate([past_rim, glu], axis=0).astype(jnp.float32)
    conv_out = jnp.zeros((tok_rows, features), jnp.float32)
    for offset in range(kernel_len):
        conv_out = (
            conv_out
            + dw_kernel[offset]
            * padded_glu[kernel_len - 1 - offset : kernel_len - 1 - offset + tok_rows]
        )
    chan_mean = tree_sum(jnp.sum(conv_out, axis=0), ("seq", "fsdp")) / all_frames
    conv_centred = conv_out - chan_mean
    chan_var = tree_sum(jnp.sum(conv_centred * conv_centred, axis=0), ("seq", "fsdp")) / all_frames
    bn_rstd = lax.rsqrt(chan_var + epsilon)
    chat = conv_centred * bn_rstd
    z_value = chat * bn_gain + bn_bias
    z_sig = jax.nn.sigmoid(z_value)
    output = (z_value * z_sig).astype(jnp.bfloat16)
    grad_z = cotangent.astype(jnp.float32) * z_sig * (1.0 + z_value * (1.0 - z_sig))
    grad_bn_bias, grad_bn_gain = tree_sum(
        (jnp.sum(grad_z, axis=0), jnp.sum(grad_z * chat, axis=0)), ("seq", "fsdp")
    )
    grad_conv = (
        bn_gain * bn_rstd * (grad_z - grad_bn_bias / all_frames - chat * grad_bn_gain / all_frames)
    )
    future_rim = from_behind(grad_conv[: kernel_len - 1], ("seq", "fsdp"), -1)
    padded_grad = jnp.concatenate([grad_conv, future_rim], axis=0)
    grad_glu = jnp.zeros((tok_rows, features), jnp.float32)
    kernel_rows = []
    for offset in range(kernel_len):
        grad_glu = grad_glu + dw_kernel[offset] * padded_grad[offset : offset + tok_rows]
        kernel_rows.append(
            jnp.sum(
                grad_conv
                * padded_glu[kernel_len - 1 - offset : kernel_len - 1 - offset + tok_rows],
                axis=0,
            )
        )
    kernel_portion = jnp.stack(kernel_rows, axis=0)
    grad_value = grad_glu * gate_sig
    grad_gate = grad_glu * value_part * gate_sig * (1.0 - gate_sig)
    grad_hidden = jnp.concatenate([grad_value, grad_gate], axis=1).astype(jnp.bfloat16)
    normalized_gradient = lax.dot_general(
        grad_hidden, full_weight, (((1,), (1,)), ((), ())), preferred_element_type=jnp.float32
    )
    grad_kernel, layer_norm_gain_gradient, grad_ln_bias = tree_sum(
        (
            kernel_portion,
            jnp.sum(normalized_gradient * standardized_input, axis=0),
            jnp.sum(normalized_gradient, axis=0),
        ),
        ("seq", "fsdp"),
    )
    rescaled_rows = normalized_gradient * layer_norm_gain
    input_gradient = row_inverse_deviation * (
        rescaled_rows
        - jnp.mean(rescaled_rows, axis=-1, keepdims=True)
        - standardized_input * jnp.mean(rescaled_rows * standardized_input, axis=-1, keepdims=True)
    )
    feature_rows = w_in.shape[0]
    group_rows = gather_own_columns(normalized_rows, "fsdp", feature_rows)
    group_grad = gather_frames(grad_hidden, "fsdp")
    row_share = lax.dot_general(
        group_rows, group_grad, (((0,), (0,)), ((), ())), preferred_element_type=jnp.float32
    )
    reduced = lax.psum_scatter(row_share, "seq", scatter_dimension=0, tiled=True)
    grad_w_in = lax.all_gather(
        reduced.astype(jnp.bfloat16), "seq", axis=0, tiled=True
    ).astype(jnp.float32)
    return (
        output,
        input_gradient.astype(jnp.bfloat16),
        grad_w_in,
        grad_kernel,
        grad_bn_gain,
        grad_bn_bias,
        layer_norm_gain_gradient,
        grad_ln_bias,
    )


def solution(mesh):
    placed = (
        P(("seq", "fsdp"), None),
        P(),
        P(),
        P("fsdp", None),
        P(),
        P(),
        P(),
        P(("seq", "fsdp"), None),
    )
    return jax.shard_map(
        on_device,
        mesh=mesh,
        in_specs=placed,
        out_specs=(
            P(("seq", "fsdp"), None),
            P(("seq", "fsdp"), None),
            P("fsdp", None),
            P(),
            P(),
            P(),
            P(),
            P(),
        ),
        check_vma=False,
    )
```

```python
import jax
import jax.numpy as jnp
from jax import lax
from jax.sharding import PartitionSpec as P

epsilon = 1e-05


def from_behind(block, axis, distance):
    devices = range(lax.axis_size(axis))
    route = [(i - distance, i) for i in devices if i - distance in devices]
    return lax.ppermute(block, axis, route)


def tree_sum(tree, axis):
    count = lax.axis_size(axis)
    if count & (count - 1):
        return lax.psum(tree, axis)
    leaves, treedef = jax.tree.flatten(tree)
    width = leaves[0].shape[-1]
    packed = jnp.concatenate([leaf.reshape(-1, width) for leaf in leaves], axis=0)
    stride = 1
    while stride < count:
        route = [(i, i ^ stride) for i in range(count)]
        packed = packed + lax.ppermute(packed, axis, route)
        stride *= 2
    out, start = [], 0
    for leaf in leaves:
        rows = leaf.size // width
        out.append(packed[start : start + rows].reshape(leaf.shape))
        start += rows
    return jax.tree.unflatten(treedef, out)


def group_shards(block, axis):
    far = lax.ppermute(block, axis, [(i, i ^ 2) for i in range(4)])
    near = lax.ppermute(
        jnp.concatenate([block, far], axis=0), axis, [(i, i ^ 1) for i in range(4)]
    )
    return jnp.concatenate([block, far, near], axis=0)


def gather_rows(block, axis):
    count = lax.axis_size(axis)
    if count != 4:
        return lax.all_gather(block, axis, axis=0, tiled=True)
    rows = block.shape[0]
    me = lax.axis_index(axis)
    shards = group_shards(block, axis)
    whole = jnp.zeros((count * rows,) + block.shape[1:], block.dtype)
    for slot, owner in enumerate((me, me ^ 2, me ^ 1, me ^ 3)):
        whole = lax.dynamic_update_slice_in_dim(
            whole, shards[slot * rows : (slot + 1) * rows], owner * rows, axis=0
        )
    return whole


def gather_own_columns(rows_block, axis, width):
    me = lax.axis_index(axis)
    frames = rows_block.shape[0]

    def cols(owner):
        return lax.dynamic_slice_in_dim(rows_block, owner * width, width, axis=1)

    if lax.axis_size(axis) != 4:
        return lax.dynamic_slice_in_dim(
            lax.all_gather(rows_block, axis, axis=0, tiled=True), me * width, width, axis=1
        )
    far = lax.ppermute(
        jnp.concatenate([cols(me ^ 2), cols(me ^ 3)], axis=0), axis, [(i, i ^ 2) for i in range(4)]
    )
    near = lax.ppermute(
        jnp.concatenate([cols(me ^ 1), far[frames:]], axis=0), axis, [(i, i ^ 1) for i in range(4)]
    )
    return jnp.concatenate([cols(me), far[:frames], near], axis=0)


def gather_frames(block, axis):
    if lax.axis_size(axis) != 4:
        return lax.all_gather(block, axis, axis=0, tiled=True)
    return group_shards(block, axis)


def on_device(
    inputs, layer_norm_gain, layer_norm_bias, w_in, dw_kernel, bn_gain, bn_bias, cotangent
):
    tok_rows = inputs.shape[0]
    features = inputs.shape[1]
    kernel_len = dw_kernel.shape[0]
    all_frames = tok_rows * lax.axis_size("seq") * lax.axis_size("fsdp")
    frames = inputs.astype(jnp.float32)
    row_mean = jnp.mean(frames, axis=-1, keepdims=True)
    centered_rows = frames - row_mean
    row_inverse_deviation = lax.rsqrt(
        jnp.mean(centered_rows * centered_rows, axis=-1, keepdims=True) + epsilon
    )
    standardized_input = centered_rows * row_inverse_deviation
    normalized_rows = (standardized_input * layer_norm_gain + layer_norm_bias).astype(jnp.bfloat16)
    full_weight = gather_rows(w_in, "fsdp")
    hidden = jnp.dot(normalized_rows, full_weight, preferred_element_type=jnp.float32)
    value_part = hidden[:, :features]
    gate_sig = jax.nn.sigmoid(hidden[:, features:])
    glu = (value_part * gate_sig).astype(jnp.bfloat16)
    past_rim = from_behind(glu[tok_rows - (kernel_len - 1) :], ("seq", "fsdp"), 1)
    padded_glu = jnp.concatenate([past_rim, glu], axis=0).astype(jnp.float32)
    conv_out = jnp.zeros((tok_rows, features), jnp.float32)
    for offset in range(kernel_len):
        conv_out = (
            conv_out
            + dw_kernel[offset]
            * padded_glu[kernel_len - 1 - offset : kernel_len - 1 - offset + tok_rows]
        )
    chan_mean = tree_sum(jnp.sum(conv_out, axis=0), ("seq", "fsdp")) / all_frames
    conv_centred = conv_out - chan_mean
    chan_var = tree_sum(jnp.sum(conv_centred * conv_centred, axis=0), ("seq", "fsdp")) / all_frames
    bn_rstd = lax.rsqrt(chan_var + epsilon)
    chat = conv_centred * bn_rstd
    z_value = chat * bn_gain + bn_bias
    z_sig = jax.nn.sigmoid(z_value)
    output = (z_value * z_sig).astype(jnp.bfloat16)
    grad_z = cotangent.astype(jnp.float32) * z_sig * (1.0 + z_value * (1.0 - z_sig))
    grad_bn_bias, grad_bn_gain = tree_sum(
        (jnp.sum(grad_z, axis=0), jnp.sum(grad_z * chat, axis=0)), ("seq", "fsdp")
    )
    grad_conv = (
        bn_gain * bn_rstd * (grad_z - grad_bn_bias / all_frames - chat * grad_bn_gain / all_frames)
    )
    future_rim = from_behind(grad_conv[: kernel_len - 1], ("seq", "fsdp"), -1)
    padded_grad = jnp.concatenate([grad_conv, future_rim], axis=0)
    grad_glu = jnp.zeros((tok_rows, features), jnp.float32)
    kernel_rows = []
    for offset in range(kernel_len):
        grad_glu = grad_glu + dw_kernel[offset] * padded_grad[offset : offset + tok_rows]
        kernel_rows.append(
            jnp.sum(
                grad_conv
                * padded_glu[kernel_len - 1 - offset : kernel_len - 1 - offset + tok_rows],
                axis=0,
            )
        )
    kernel_portion = jnp.stack(kernel_rows, axis=0)
    grad_value = grad_glu * gate_sig
    grad_gate = grad_glu * value_part * gate_sig * (1.0 - gate_sig)
    grad_hidden = jnp.concatenate([grad_value, grad_gate], axis=1).astype(jnp.bfloat16)
    normalized_gradient = lax.dot_general(
        grad_hidden, full_weight, (((1,), (1,)), ((), ())), preferred_element_type=jnp.float32
    )
    rescaled_rows = normalized_gradient * layer_norm_gain
    input_gradient = row_inverse_deviation * (
        rescaled_rows
        - jnp.mean(rescaled_rows, axis=-1, keepdims=True)
        - standardized_input * jnp.mean(rescaled_rows * standardized_input, axis=-1, keepdims=True)
    )
    local_sums = (
        kernel_portion,
        jnp.sum(normalized_gradient * standardized_input, axis=0),
        jnp.sum(normalized_gradient, axis=0),
    )
    feature_rows = w_in.shape[0]
    group_rows = gather_own_columns(normalized_rows, "fsdp", feature_rows)
    halves = [grad_hidden[:, :features], grad_hidden[:, features:]]
    grad_w_parts = []
    if lax.axis_size("fsdp") == 4:
        cross = [(i, i ^ 2) for i in range(4)]
        on_chip = [(i, i ^ 1) for i in range(4)]
        first_far = lax.ppermute(halves[0], "fsdp", cross)
        first_far, input_gradient, local_sums = lax.optimization_barrier(
            (first_far, input_gradient, local_sums)
        )
        second_half, first_far = lax.optimization_barrier((halves[1], first_far))
        second_far = lax.ppermute(second_half, "fsdp", cross)
        group_grads = []
        for half, far in ((halves[0], first_far), (second_half, second_far)):
            near = lax.ppermute(jnp.concatenate([half, far], axis=0), "fsdp", on_chip)
            group_grads.append(jnp.concatenate([half, far, near], axis=0))
    else:
        group_grads = [lax.all_gather(h, "fsdp", axis=0, tiled=True) for h in halves]
    for group_grad in group_grads:
        row_share = lax.dot_general(
            group_rows, group_grad, (((0,), (0,)), ((), ())), preferred_element_type=jnp.float32
        )
        reduced = lax.psum_scatter(row_share, "seq", scatter_dimension=0, tiled=True)
        grad_w_parts.append(
            lax.all_gather(reduced.astype(jnp.bfloat16), "seq", axis=0, tiled=True)
        )
    grad_w_in = jnp.concatenate(grad_w_parts, axis=1).astype(jnp.float32)
    grad_kernel, layer_norm_gain_gradient, grad_ln_bias = tree_sum(local_sums, ("seq", "fsdp"))
    return (
        output,
        input_gradient.astype(jnp.bfloat16),
        grad_w_in,
        grad_kernel,
        grad_bn_gain,
        grad_bn_bias,
        layer_norm_gain_gradient,
        grad_ln_bias,
    )


def solution(mesh):
    placed = (
        P(("seq", "fsdp"), None),
        P(),
        P(),
        P("fsdp", None),
        P(),
        P(),
        P(),
        P(("seq", "fsdp"), None),
    )
    return jax.shard_map(
        on_device,
        mesh=mesh,
        in_specs=placed,
        out_specs=(
            P(("seq", "fsdp"), None),
            P(("seq", "fsdp"), None),
            P("fsdp", None),
            P(),
            P(),
            P(),
            P(),
            P(),
        ),
        check_vma=False,
    )
```

```python
import jax
import jax.numpy as jnp
from jax import lax
from jax.sharding import PartitionSpec as P

epsilon = 1e-05


def from_behind(block, axis, distance):
    devices = range(lax.axis_size(axis))
    route = [(i - distance, i) for i in devices if i - distance in devices]
    return lax.ppermute(block, axis, route)


def tree_sum(tree, axis):
    count = lax.axis_size(axis)
    if count & (count - 1):
        return lax.psum(tree, axis)
    leaves, treedef = jax.tree.flatten(tree)
    width = leaves[0].shape[-1]
    packed = jnp.concatenate([leaf.reshape(-1, width) for leaf in leaves], axis=0)
    stride = 1
    while stride < count:
        route = [(i, i ^ stride) for i in range(count)]
        packed = packed + lax.ppermute(packed, axis, route)
        stride *= 2
    out, start = [], 0
    for leaf in leaves:
        rows = leaf.size // width
        out.append(packed[start : start + rows].reshape(leaf.shape))
        start += rows
    return jax.tree.unflatten(treedef, out)


def group_shards(block, axis):
    far = lax.ppermute(block, axis, [(i, i ^ 2) for i in range(4)])
    near = lax.ppermute(
        jnp.concatenate([block, far], axis=0), axis, [(i, i ^ 1) for i in range(4)]
    )
    return jnp.concatenate([block, far, near], axis=0)


def gather_rows(block, axis):
    count = lax.axis_size(axis)
    if count != 4:
        return lax.all_gather(block, axis, axis=0, tiled=True)
    rows = block.shape[0]
    me = lax.axis_index(axis)
    shards = group_shards(block, axis)
    whole = jnp.zeros((count * rows,) + block.shape[1:], block.dtype)
    for slot, owner in enumerate((me, me ^ 2, me ^ 1, me ^ 3)):
        whole = lax.dynamic_update_slice_in_dim(
            whole, shards[slot * rows : (slot + 1) * rows], owner * rows, axis=0
        )
    return whole


def gather_own_columns(rows_block, axis, width):
    me = lax.axis_index(axis)
    frames = rows_block.shape[0]

    def cols(owner):
        return lax.dynamic_slice_in_dim(rows_block, owner * width, width, axis=1)

    if lax.axis_size(axis) != 4:
        return lax.dynamic_slice_in_dim(
            lax.all_gather(rows_block, axis, axis=0, tiled=True), me * width, width, axis=1
        )
    far = lax.ppermute(
        jnp.concatenate([cols(me ^ 2), cols(me ^ 3)], axis=0), axis, [(i, i ^ 2) for i in range(4)]
    )
    near = lax.ppermute(
        jnp.concatenate([cols(me ^ 1), far[frames:]], axis=0), axis, [(i, i ^ 1) for i in range(4)]
    )
    return jnp.concatenate([cols(me), far[:frames], near], axis=0)


def gather_frames(block, axis):
    if lax.axis_size(axis) != 4:
        return lax.all_gather(block, axis, axis=0, tiled=True)
    return group_shards(block, axis)


def on_device(
    inputs, layer_norm_gain, layer_norm_bias, w_in, dw_kernel, bn_gain, bn_bias, cotangent
):
    tok_rows = inputs.shape[0]
    features = inputs.shape[1]
    kernel_len = dw_kernel.shape[0]
    all_frames = tok_rows * lax.axis_size("seq") * lax.axis_size("fsdp")
    frames = inputs.astype(jnp.float32)
    row_mean = jnp.mean(frames, axis=-1, keepdims=True)
    centered_rows = frames - row_mean
    row_inverse_deviation = lax.rsqrt(
        jnp.mean(centered_rows * centered_rows, axis=-1, keepdims=True) + epsilon
    )
    standardized_input = centered_rows * row_inverse_deviation
    normalized_rows = (standardized_input * layer_norm_gain + layer_norm_bias).astype(jnp.bfloat16)
    full_weight = gather_rows(w_in, "fsdp")
    hidden = jnp.dot(normalized_rows, full_weight, preferred_element_type=jnp.float32)
    value_part = hidden[:, :features]
    gate_sig = jax.nn.sigmoid(hidden[:, features:])
    glu = (value_part * gate_sig).astype(jnp.bfloat16)
    past_rim = from_behind(glu[tok_rows - (kernel_len - 1) :], ("seq", "fsdp"), 1)
    padded_glu = jnp.concatenate([past_rim, glu], axis=0).astype(jnp.float32)
    conv_out = jnp.zeros((tok_rows, features), jnp.float32)
    for offset in range(kernel_len):
        conv_out = (
            conv_out
            + dw_kernel[offset]
            * padded_glu[kernel_len - 1 - offset : kernel_len - 1 - offset + tok_rows]
        )
    chan_mean = tree_sum(jnp.sum(conv_out, axis=0), ("seq", "fsdp")) / all_frames
    conv_centred = conv_out - chan_mean
    chan_var = tree_sum(jnp.sum(conv_centred * conv_centred, axis=0), ("seq", "fsdp")) / all_frames
    bn_rstd = lax.rsqrt(chan_var + epsilon)
    chat = conv_centred * bn_rstd
    z_value = chat * bn_gain + bn_bias
    z_sig = jax.nn.sigmoid(z_value)
    output = (z_value * z_sig).astype(jnp.bfloat16)
    grad_z = cotangent.astype(jnp.float32) * z_sig * (1.0 + z_value * (1.0 - z_sig))
    grad_bn_bias, grad_bn_gain = tree_sum(
        (jnp.sum(grad_z, axis=0), jnp.sum(grad_z * chat, axis=0)), ("seq", "fsdp")
    )
    grad_conv = (
        bn_gain * bn_rstd * (grad_z - grad_bn_bias / all_frames - chat * grad_bn_gain / all_frames)
    )
    future_rim = from_behind(grad_conv[: kernel_len - 1], ("seq", "fsdp"), -1)
    padded_grad = jnp.concatenate([grad_conv, future_rim], axis=0)
    grad_glu = jnp.zeros((tok_rows, features), jnp.float32)
    kernel_rows = []
    for offset in range(kernel_len):
        grad_glu = grad_glu + dw_kernel[offset] * padded_grad[offset : offset + tok_rows]
        kernel_rows.append(
            jnp.sum(
                grad_conv
                * padded_glu[kernel_len - 1 - offset : kernel_len - 1 - offset + tok_rows],
                axis=0,
            )
        )
    kernel_portion = jnp.stack(kernel_rows, axis=0)
    grad_value = grad_glu * gate_sig
    grad_gate = grad_glu * value_part * gate_sig * (1.0 - gate_sig)
    grad_hidden = jnp.concatenate([grad_value, grad_gate], axis=1).astype(jnp.bfloat16)
    normalized_gradient = lax.dot_general(
        grad_hidden, full_weight, (((1,), (1,)), ((), ())), preferred_element_type=jnp.float32
    )
    rescaled_rows = normalized_gradient * layer_norm_gain
    input_gradient = row_inverse_deviation * (
        rescaled_rows
        - jnp.mean(rescaled_rows, axis=-1, keepdims=True)
        - standardized_input * jnp.mean(rescaled_rows * standardized_input, axis=-1, keepdims=True)
    )
    local_sums = (
        kernel_portion,
        jnp.sum(normalized_gradient * standardized_input, axis=0),
        jnp.sum(normalized_gradient, axis=0),
    )
    feature_rows = w_in.shape[0]
    group_rows = gather_own_columns(normalized_rows, "fsdp", feature_rows)
    if lax.axis_size("fsdp") == 4:
        far = lax.ppermute(grad_hidden, "fsdp", [(i, i ^ 2) for i in range(4)])
        far, input_gradient, local_sums = lax.optimization_barrier(
            (far, input_gradient, local_sums)
        )
        near = lax.ppermute(
            jnp.concatenate([grad_hidden, far], axis=0), "fsdp", [(i, i ^ 1) for i in range(4)]
        )
        group_grad = jnp.concatenate([grad_hidden, far, near], axis=0)
    else:
        group_grad = lax.all_gather(grad_hidden, "fsdp", axis=0, tiled=True)
    row_share = lax.dot_general(
        group_rows, group_grad, (((0,), (0,)), ((), ())), preferred_element_type=jnp.float32
    )
    reduced = lax.psum_scatter(row_share, "seq", scatter_dimension=0, tiled=True)
    grad_w_in = lax.all_gather(
        reduced.astype(jnp.bfloat16), "seq", axis=0, tiled=True
    ).astype(jnp.float32)
    grad_kernel, layer_norm_gain_gradient, grad_ln_bias = tree_sum(local_sums, ("seq", "fsdp"))
    return (
        output,
        input_gradient.astype(jnp.bfloat16),
        grad_w_in,
        grad_kernel,
        grad_bn_gain,
        grad_bn_bias,
        layer_norm_gain_gradient,
        grad_ln_bias,
    )


def solution(mesh):
    placed = (
        P(("seq", "fsdp"), None),
        P(),
        P(),
        P("fsdp", None),
        P(),
        P(),
        P(),
        P(("seq", "fsdp"), None),
    )
    return jax.shard_map(
        on_device,
        mesh=mesh,
        in_specs=placed,
        out_specs=(
            P(("seq", "fsdp"), None),
            P(("seq", "fsdp"), None),
            P("fsdp", None),
            P(),
            P(),
            P(),
            P(),
            P(),
        ),
        check_vma=False,
    )
```

```python
import jax
import jax.numpy as jnp
from jax import lax
from jax.sharding import PartitionSpec as P

epsilon = 1e-05


def from_behind(block, axis, distance):
    devices = range(lax.axis_size(axis))
    route = [(i - distance, i) for i in devices if i - distance in devices]
    return lax.ppermute(block, axis, route)


def tree_sum(tree, axis):
    count = lax.axis_size(axis)
    if count & (count - 1):
        return lax.psum(tree, axis)
    leaves, treedef = jax.tree.flatten(tree)
    width = leaves[0].shape[-1]
    packed = jnp.concatenate([leaf.reshape(-1, width) for leaf in leaves], axis=0)
    stride = 1
    while stride < count:
        route = [(i, i ^ stride) for i in range(count)]
        packed = packed + lax.ppermute(packed, axis, route)
        stride *= 2
    out, start = [], 0
    for leaf in leaves:
        rows = leaf.size // width
        out.append(packed[start : start + rows].reshape(leaf.shape))
        start += rows
    return jax.tree.unflatten(treedef, out)


def group_shards(block, axis):
    far = lax.ppermute(block, axis, [(i, i ^ 2) for i in range(4)])
    near = lax.ppermute(block, axis, [(i, i ^ 1) for i in range(4)])
    near_far = lax.ppermute(far, axis, [(i, i ^ 1) for i in range(4)])
    return [block, far, near, near_far]


def gather_rows(block, axis):
    count = lax.axis_size(axis)
    if count != 4:
        return lax.all_gather(block, axis, axis=0, tiled=True)
    rows = block.shape[0]
    me = lax.axis_index(axis)
    shards = group_shards(block, axis)
    whole = jnp.zeros((count * rows,) + block.shape[1:], block.dtype)
    for shard, owner in zip(shards, (me, me ^ 2, me ^ 1, me ^ 3)):
        whole = lax.dynamic_update_slice_in_dim(whole, shard, owner * rows, axis=0)
    return whole


def gather_own_columns(rows_block, axis, width):
    me = lax.axis_index(axis)
    frames = rows_block.shape[0]

    def cols(owner):
        return lax.dynamic_slice_in_dim(rows_block, owner * width, width, axis=1)

    if lax.axis_size(axis) != 4:
        return lax.dynamic_slice_in_dim(
            lax.all_gather(rows_block, axis, axis=0, tiled=True), me * width, width, axis=1
        )
    far = lax.ppermute(
        jnp.concatenate([cols(me ^ 2), cols(me ^ 3)], axis=0), axis, [(i, i ^ 2) for i in range(4)]
    )
    near = lax.ppermute(
        jnp.concatenate([cols(me ^ 1), far[frames:]], axis=0), axis, [(i, i ^ 1) for i in range(4)]
    )
    return jnp.concatenate([cols(me), far[:frames], near], axis=0)


def on_device(
    inputs, layer_norm_gain, layer_norm_bias, w_in, dw_kernel, bn_gain, bn_bias, cotangent
):
    tok_rows = inputs.shape[0]
    features = inputs.shape[1]
    kernel_len = dw_kernel.shape[0]
    all_frames = tok_rows * lax.axis_size("seq") * lax.axis_size("fsdp")
    frames = inputs.astype(jnp.float32)
    row_mean = jnp.mean(frames, axis=-1, keepdims=True)
    centered_rows = frames - row_mean
    row_inverse_deviation = lax.rsqrt(
        jnp.mean(centered_rows * centered_rows, axis=-1, keepdims=True) + epsilon
    )
    standardized_input = centered_rows * row_inverse_deviation
    normalized_rows = (standardized_input * layer_norm_gain + layer_norm_bias).astype(jnp.bfloat16)
    full_weight = gather_rows(w_in, "fsdp")
    hidden = jnp.dot(normalized_rows, full_weight, preferred_element_type=jnp.float32)
    value_part = hidden[:, :features]
    gate_sig = jax.nn.sigmoid(hidden[:, features:])
    glu = (value_part * gate_sig).astype(jnp.bfloat16)
    past_rim = from_behind(glu[tok_rows - (kernel_len - 1) :], ("seq", "fsdp"), 1)
    padded_glu = jnp.concatenate([past_rim, glu], axis=0).astype(jnp.float32)
    conv_out = jnp.zeros((tok_rows, features), jnp.float32)
    for offset in range(kernel_len):
        conv_out = (
            conv_out
            + dw_kernel[offset]
            * padded_glu[kernel_len - 1 - offset : kernel_len - 1 - offset + tok_rows]
        )
    chan_mean = tree_sum(jnp.sum(conv_out, axis=0), ("seq", "fsdp")) / all_frames
    conv_centred = conv_out - chan_mean
    chan_var = tree_sum(jnp.sum(conv_centred * conv_centred, axis=0), ("seq", "fsdp")) / all_frames
    bn_rstd = lax.rsqrt(chan_var + epsilon)
    chat = conv_centred * bn_rstd
    z_value = chat * bn_gain + bn_bias
    z_sig = jax.nn.sigmoid(z_value)
    output = (z_value * z_sig).astype(jnp.bfloat16)
    grad_z = cotangent.astype(jnp.float32) * z_sig * (1.0 + z_value * (1.0 - z_sig))
    grad_bn_bias, grad_bn_gain = tree_sum(
        (jnp.sum(grad_z, axis=0), jnp.sum(grad_z * chat, axis=0)), ("seq", "fsdp")
    )
    grad_conv = (
        bn_gain * bn_rstd * (grad_z - grad_bn_bias / all_frames - chat * grad_bn_gain / all_frames)
    )
    future_rim = from_behind(grad_conv[: kernel_len - 1], ("seq", "fsdp"), -1)
    padded_grad = jnp.concatenate([grad_conv, future_rim], axis=0)
    grad_glu = jnp.zeros((tok_rows, features), jnp.float32)
    kernel_rows = []
    for offset in range(kernel_len):
        grad_glu = grad_glu + dw_kernel[offset] * padded_grad[offset : offset + tok_rows]
        kernel_rows.append(
            jnp.sum(
                grad_conv
                * padded_glu[kernel_len - 1 - offset : kernel_len - 1 - offset + tok_rows],
                axis=0,
            )
        )
    kernel_portion = jnp.stack(kernel_rows, axis=0)
    grad_value = grad_glu * gate_sig
    grad_gate = grad_glu * value_part * gate_sig * (1.0 - gate_sig)
    grad_hidden = jnp.concatenate([grad_value, grad_gate], axis=1).astype(jnp.bfloat16)
    normalized_gradient = lax.dot_general(
        grad_hidden, full_weight, (((1,), (1,)), ((), ())), preferred_element_type=jnp.float32
    )
    rescaled_rows = normalized_gradient * layer_norm_gain
    input_gradient = row_inverse_deviation * (
        rescaled_rows
        - jnp.mean(rescaled_rows, axis=-1, keepdims=True)
        - standardized_input * jnp.mean(rescaled_rows * standardized_input, axis=-1, keepdims=True)
    )
    local_sums = (
        kernel_portion,
        jnp.sum(normalized_gradient * standardized_input, axis=0),
        jnp.sum(normalized_gradient, axis=0),
    )
    feature_rows = w_in.shape[0]
    group_rows = gather_own_columns(normalized_rows, "fsdp", feature_rows)
    contract = (((0,), (0,)), ((), ()))
    if lax.axis_size("fsdp") == 4:
        far = lax.ppermute(grad_hidden, "fsdp", [(i, i ^ 2) for i in range(4)])
        near = lax.ppermute(grad_hidden, "fsdp", [(i, i ^ 1) for i in range(4)])
        far, input_gradient, local_sums = lax.optimization_barrier(
            (far, input_gradient, local_sums)
        )
        near_far = lax.ppermute(far, "fsdp", [(i, i ^ 1) for i in range(4)])
        pieces = (grad_hidden, far, near, near_far)
        row_share = None
        for slot, piece in enumerate(pieces):
            term = lax.dot_general(
                group_rows[slot * tok_rows : (slot + 1) * tok_rows],
                piece,
                contract,
                preferred_element_type=jnp.float32,
            )
            row_share = term if row_share is None else row_share + term
    else:
        group_grad = lax.all_gather(grad_hidden, "fsdp", axis=0, tiled=True)
        row_share = lax.dot_general(
            group_rows, group_grad, contract, preferred_element_type=jnp.float32
        )
    reduced = lax.psum_scatter(row_share, "seq", scatter_dimension=0, tiled=True)
    grad_w_in = lax.all_gather(
        reduced.astype(jnp.bfloat16), "seq", axis=0, tiled=True
    ).astype(jnp.float32)
    grad_kernel, layer_norm_gain_gradient, grad_ln_bias = tree_sum(local_sums, ("seq", "fsdp"))
    return (
        output,
        input_gradient.astype(jnp.bfloat16),
        grad_w_in,
        grad_kernel,
        grad_bn_gain,
        grad_bn_bias,
        layer_norm_gain_gradient,
        grad_ln_bias,
    )


def solution(mesh):
    placed = (
        P(("seq", "fsdp"), None),
        P(),
        P(),
        P("fsdp", None),
        P(),
        P(),
        P(),
        P(("seq", "fsdp"), None),
    )
    return jax.shard_map(
        on_device,
        mesh=mesh,
        in_specs=placed,
        out_specs=(
            P(("seq", "fsdp"), None),
            P(("seq", "fsdp"), None),
            P("fsdp", None),
            P(),
            P(),
            P(),
            P(),
            P(),
        ),
        check_vma=False,
    )
```

```python
import jax
import jax.numpy as jnp
from jax import lax
from jax.sharding import PartitionSpec as P

epsilon = 1e-05


def from_behind(block, axis, distance):
    devices = range(lax.axis_size(axis))
    route = [(i - distance, i) for i in devices if i - distance in devices]
    return lax.ppermute(block, axis, route)


def tree_sum(tree, axis):
    count = lax.axis_size(axis)
    if count & (count - 1):
        return lax.psum(tree, axis)
    leaves, treedef = jax.tree.flatten(tree)
    width = leaves[0].shape[-1]
    packed = jnp.concatenate([leaf.reshape(-1, width) for leaf in leaves], axis=0)
    stride = 1
    while stride < count:
        route = [(i, i ^ stride) for i in range(count)]
        packed = packed + lax.ppermute(packed, axis, route)
        stride *= 2
    out, start = [], 0
    for leaf in leaves:
        rows = leaf.size // width
        out.append(packed[start : start + rows].reshape(leaf.shape))
        start += rows
    return jax.tree.unflatten(treedef, out)


def mean_and_var(block, axis):
    count = lax.axis_size(axis)
    frames = block.shape[0]
    if count & (count - 1):
        total = count * frames
        mean = lax.psum(jnp.sum(block, axis=0), axis) / total
        centred = block - mean
        return mean, lax.psum(jnp.sum(centred * centred, axis=0), axis) / total
    mean = jnp.mean(block, axis=0)
    centred = block - mean
    spread = jnp.sum(centred * centred, axis=0)
    stats = jnp.stack([mean, spread])
    rows, stride = frames, 1
    while stride < count:
        other = lax.ppermute(stats, axis, [(i, i ^ stride) for i in range(count)])
        delta = stats[0] - other[0]
        stats = jnp.stack(
            [
                (stats[0] + other[0]) * 0.5,
                (stats[1] + other[1]) + (0.5 * rows) * (delta * delta),
            ]
        )
        rows, stride = rows * 2, stride * 2
    return stats[0], stats[1] / rows


def group_shards(block, axis):
    far = lax.ppermute(block, axis, [(i, i ^ 2) for i in range(4)])
    near = lax.ppermute(block, axis, [(i, i ^ 1) for i in range(4)])
    near_far = lax.ppermute(far, axis, [(i, i ^ 1) for i in range(4)])
    return [block, far, near, near_far]


def gather_rows(block, axis):
    count = lax.axis_size(axis)
    if count != 4:
        return lax.all_gather(block, axis, axis=0, tiled=True)
    rows = block.shape[0]
    me = lax.axis_index(axis)
    shards = group_shards(block, axis)
    whole = jnp.zeros((count * rows,) + block.shape[1:], block.dtype)
    for shard, owner in zip(shards, (me, me ^ 2, me ^ 1, me ^ 3)):
        whole = lax.dynamic_update_slice_in_dim(whole, shard, owner * rows, axis=0)
    return whole


def gather_own_columns(rows_block, axis, width):
    me = lax.axis_index(axis)
    frames = rows_block.shape[0]

    def cols(owner):
        return lax.dynamic_slice_in_dim(rows_block, owner * width, width, axis=1)

    if lax.axis_size(axis) != 4:
        return lax.dynamic_slice_in_dim(
            lax.all_gather(rows_block, axis, axis=0, tiled=True), me * width, width, axis=1
        )
    far = lax.ppermute(
        jnp.concatenate([cols(me ^ 2), cols(me ^ 3)], axis=0), axis, [(i, i ^ 2) for i in range(4)]
    )
    near = lax.ppermute(
        jnp.concatenate([cols(me ^ 1), far[frames:]], axis=0), axis, [(i, i ^ 1) for i in range(4)]
    )
    return jnp.concatenate([cols(me), far[:frames], near], axis=0)


def on_device(
    inputs, layer_norm_gain, layer_norm_bias, w_in, dw_kernel, bn_gain, bn_bias, cotangent
):
    tok_rows = inputs.shape[0]
    features = inputs.shape[1]
    kernel_len = dw_kernel.shape[0]
    all_frames = tok_rows * lax.axis_size("seq") * lax.axis_size("fsdp")
    frames = inputs.astype(jnp.float32)
    row_mean = jnp.mean(frames, axis=-1, keepdims=True)
    centered_rows = frames - row_mean
    row_inverse_deviation = lax.rsqrt(
        jnp.mean(centered_rows * centered_rows, axis=-1, keepdims=True) + epsilon
    )
    standardized_input = centered_rows * row_inverse_deviation
    normalized_rows = (standardized_input * layer_norm_gain + layer_norm_bias).astype(jnp.bfloat16)
    full_weight = gather_rows(w_in, "fsdp")
    hidden = jnp.dot(normalized_rows, full_weight, preferred_element_type=jnp.float32)
    value_part = hidden[:, :features]
    gate_sig = jax.nn.sigmoid(hidden[:, features:])
    glu = (value_part * gate_sig).astype(jnp.bfloat16)
    past_rim = from_behind(glu[tok_rows - (kernel_len - 1) :], ("seq", "fsdp"), 1)
    padded_glu = jnp.concatenate([past_rim, glu], axis=0).astype(jnp.float32)
    conv_out = jnp.zeros((tok_rows, features), jnp.float32)
    for offset in range(kernel_len):
        conv_out = (
            conv_out
            + dw_kernel[offset]
            * padded_glu[kernel_len - 1 - offset : kernel_len - 1 - offset + tok_rows]
        )
    chan_mean, chan_var = mean_and_var(conv_out, ("seq", "fsdp"))
    conv_centred = conv_out - chan_mean
    bn_rstd = lax.rsqrt(chan_var + epsilon)
    chat = conv_centred * bn_rstd
    z_value = chat * bn_gain + bn_bias
    z_sig = jax.nn.sigmoid(z_value)
    output = (z_value * z_sig).astype(jnp.bfloat16)
    grad_z = cotangent.astype(jnp.float32) * z_sig * (1.0 + z_value * (1.0 - z_sig))
    grad_bn_bias, grad_bn_gain = tree_sum(
        (jnp.sum(grad_z, axis=0), jnp.sum(grad_z * chat, axis=0)), ("seq", "fsdp")
    )
    grad_conv = (
        bn_gain * bn_rstd * (grad_z - grad_bn_bias / all_frames - chat * grad_bn_gain / all_frames)
    )
    future_rim = from_behind(grad_conv[: kernel_len - 1], ("seq", "fsdp"), -1)
    padded_grad = jnp.concatenate([grad_conv, future_rim], axis=0)
    grad_glu = jnp.zeros((tok_rows, features), jnp.float32)
    kernel_rows = []
    for offset in range(kernel_len):
        grad_glu = grad_glu + dw_kernel[offset] * padded_grad[offset : offset + tok_rows]
        kernel_rows.append(
            jnp.sum(
                grad_conv
                * padded_glu[kernel_len - 1 - offset : kernel_len - 1 - offset + tok_rows],
                axis=0,
            )
        )
    kernel_portion = jnp.stack(kernel_rows, axis=0)
    grad_value = grad_glu * gate_sig
    grad_gate = grad_glu * value_part * gate_sig * (1.0 - gate_sig)
    grad_hidden = jnp.concatenate([grad_value, grad_gate], axis=1).astype(jnp.bfloat16)
    normalized_gradient = lax.dot_general(
        grad_hidden, full_weight, (((1,), (1,)), ((), ())), preferred_element_type=jnp.float32
    )
    rescaled_rows = normalized_gradient * layer_norm_gain
    input_gradient = row_inverse_deviation * (
        rescaled_rows
        - jnp.mean(rescaled_rows, axis=-1, keepdims=True)
        - standardized_input * jnp.mean(rescaled_rows * standardized_input, axis=-1, keepdims=True)
    )
    local_sums = (
        kernel_portion,
        jnp.sum(normalized_gradient * standardized_input, axis=0),
        jnp.sum(normalized_gradient, axis=0),
    )
    feature_rows = w_in.shape[0]
    group_rows = gather_own_columns(normalized_rows, "fsdp", feature_rows)
    contract = (((0,), (0,)), ((), ()))
    if lax.axis_size("fsdp") == 4:
        far = lax.ppermute(grad_hidden, "fsdp", [(i, i ^ 2) for i in range(4)])
        near = lax.ppermute(grad_hidden, "fsdp", [(i, i ^ 1) for i in range(4)])
        far, input_gradient, local_sums = lax.optimization_barrier(
            (far, input_gradient, local_sums)
        )
        near_far = lax.ppermute(far, "fsdp", [(i, i ^ 1) for i in range(4)])
        pieces = (grad_hidden, far, near, near_far)
        row_share = None
        for slot, piece in enumerate(pieces):
            term = lax.dot_general(
                group_rows[slot * tok_rows : (slot + 1) * tok_rows],
                piece,
                contract,
                preferred_element_type=jnp.float32,
            )
            row_share = term if row_share is None else row_share + term
    else:
        group_grad = lax.all_gather(grad_hidden, "fsdp", axis=0, tiled=True)
        row_share = lax.dot_general(
            group_rows, group_grad, contract, preferred_element_type=jnp.float32
        )
    reduced = lax.psum_scatter(row_share, "seq", scatter_dimension=0, tiled=True)
    grad_w_in = lax.all_gather(
        reduced.astype(jnp.bfloat16), "seq", axis=0, tiled=True
    ).astype(jnp.float32)
    grad_kernel, layer_norm_gain_gradient, grad_ln_bias = tree_sum(local_sums, ("seq", "fsdp"))
    return (
        output,
        input_gradient.astype(jnp.bfloat16),
        grad_w_in,
        grad_kernel,
        grad_bn_gain,
        grad_bn_bias,
        layer_norm_gain_gradient,
        grad_ln_bias,
    )


def solution(mesh):
    placed = (
        P(("seq", "fsdp"), None),
        P(),
        P(),
        P("fsdp", None),
        P(),
        P(),
        P(),
        P(("seq", "fsdp"), None),
    )
    return jax.shard_map(
        on_device,
        mesh=mesh,
        in_specs=placed,
        out_specs=(
            P(("seq", "fsdp"), None),
            P(("seq", "fsdp"), None),
            P("fsdp", None),
            P(),
            P(),
            P(),
            P(),
            P(),
        ),
        check_vma=False,
    )
```

```python
import jax
import jax.numpy as jnp
from jax import lax
from jax.sharding import PartitionSpec as P

epsilon = 1e-05


def from_behind(block, axis, distance):
    devices = range(lax.axis_size(axis))
    route = [(i - distance, i) for i in devices if i - distance in devices]
    return lax.ppermute(block, axis, route)


def tree_sum(tree, axis):
    count = lax.axis_size(axis)
    if count & (count - 1):
        return lax.psum(tree, axis)
    leaves, treedef = jax.tree.flatten(tree)
    width = leaves[0].shape[-1]
    packed = jnp.concatenate([leaf.reshape(-1, width) for leaf in leaves], axis=0)
    stride = 1
    while stride < count:
        route = [(i, i ^ stride) for i in range(count)]
        packed = packed + lax.ppermute(packed, axis, route)
        stride *= 2
    out, start = [], 0
    for leaf in leaves:
        rows = leaf.size // width
        out.append(packed[start : start + rows].reshape(leaf.shape))
        start += rows
    return jax.tree.unflatten(treedef, out)


def exchange(x, axis):
    count = lax.axis_size(axis)
    got = [x] + [
        lax.ppermute(x, axis, [(i, i ^ k) for i in range(count)]) for k in range(1, count)
    ]
    return jnp.take(jnp.stack(got), lax.axis_index(axis) ^ jnp.arange(count), axis=0)


def combine(x, axes, merge, rows):
    for axis in axes:
        count = lax.axis_size(axis)
        if count in (2, 4, 8):
            items = list(exchange(x, axis))
            while len(items) > 1:
                items = [merge(items[j], items[j + 1], rows) for j in range(0, len(items), 2)]
                rows *= 2
            x = items[0]
        else:
            stride = 1
            while stride < count:
                other = lax.ppermute(x, axis, [(i, i ^ stride) for i in range(count)])
                x = merge(x, other, rows)
                rows, stride = rows * 2, stride * 2
    return x, rows


def pair_stats(a, b, rows):
    delta = a[0] - b[0]
    return jnp.stack([(a[0] + b[0]) * 0.5, (a[1] + b[1]) + (0.5 * rows) * (delta * delta)])


def mean_and_var(block, axes):
    if any(lax.axis_size(a) & (lax.axis_size(a) - 1) for a in axes):
        total = block.shape[0] * lax.axis_size(axes)
        mean = lax.psum(jnp.sum(block, axis=0), axes) / total
        centred = block - mean
        return mean, lax.psum(jnp.sum(centred * centred, axis=0), axes) / total
    mean = jnp.mean(block, axis=0)
    centred = block - mean
    stats, rows = combine(
        jnp.stack([mean, jnp.sum(centred * centred, axis=0)]), axes, pair_stats, block.shape[0]
    )
    return stats[0], stats[1] / rows


def fast_sum(tree, axes):
    if any(lax.axis_size(a) & (lax.axis_size(a) - 1) for a in axes):
        return lax.psum(tree, axes)
    leaves, treedef = jax.tree.flatten(tree)
    width = leaves[0].shape[-1]
    packed = jnp.concatenate([leaf.reshape(-1, width) for leaf in leaves], axis=0)
    packed, _ = combine(packed, axes, lambda a, b, rows: a + b, 1)
    out, start = [], 0
    for leaf in leaves:
        count = leaf.size // width
        out.append(packed[start : start + count].reshape(leaf.shape))
        start += count
    return jax.tree.unflatten(treedef, out)


def group_shards(block, axis):
    far = lax.ppermute(block, axis, [(i, i ^ 2) for i in range(4)])
    near = lax.ppermute(block, axis, [(i, i ^ 1) for i in range(4)])
    near_far = lax.ppermute(far, axis, [(i, i ^ 1) for i in range(4)])
    return [block, far, near, near_far]


def gather_rows(block, axis):
    count = lax.axis_size(axis)
    if count != 4:
        return lax.all_gather(block, axis, axis=0, tiled=True)
    rows = block.shape[0]
    me = lax.axis_index(axis)
    shards = group_shards(block, axis)
    whole = jnp.zeros((count * rows,) + block.shape[1:], block.dtype)
    for shard, owner in zip(shards, (me, me ^ 2, me ^ 1, me ^ 3)):
        whole = lax.dynamic_update_slice_in_dim(whole, shard, owner * rows, axis=0)
    return whole


def gather_own_columns(rows_block, axis, width):
    me = lax.axis_index(axis)
    frames = rows_block.shape[0]

    def cols(owner):
        return lax.dynamic_slice_in_dim(rows_block, owner * width, width, axis=1)

    if lax.axis_size(axis) != 4:
        return lax.dynamic_slice_in_dim(
            lax.all_gather(rows_block, axis, axis=0, tiled=True), me * width, width, axis=1
        )
    far = lax.ppermute(
        jnp.concatenate([cols(me ^ 2), cols(me ^ 3)], axis=0), axis, [(i, i ^ 2) for i in range(4)]
    )
    near = lax.ppermute(
        jnp.concatenate([cols(me ^ 1), far[frames:]], axis=0), axis, [(i, i ^ 1) for i in range(4)]
    )
    return jnp.concatenate([cols(me), far[:frames], near], axis=0)


def on_device(
    inputs, layer_norm_gain, layer_norm_bias, w_in, dw_kernel, bn_gain, bn_bias, cotangent
):
    tok_rows = inputs.shape[0]
    features = inputs.shape[1]
    kernel_len = dw_kernel.shape[0]
    all_frames = tok_rows * lax.axis_size("seq") * lax.axis_size("fsdp")
    frames = inputs.astype(jnp.float32)
    row_mean = jnp.mean(frames, axis=-1, keepdims=True)
    centered_rows = frames - row_mean
    row_inverse_deviation = lax.rsqrt(
        jnp.mean(centered_rows * centered_rows, axis=-1, keepdims=True) + epsilon
    )
    standardized_input = centered_rows * row_inverse_deviation
    normalized_rows = (standardized_input * layer_norm_gain + layer_norm_bias).astype(jnp.bfloat16)
    full_weight = gather_rows(w_in, "fsdp")
    hidden = jnp.dot(normalized_rows, full_weight, preferred_element_type=jnp.float32)
    value_part = hidden[:, :features]
    gate_sig = jax.nn.sigmoid(hidden[:, features:])
    glu = (value_part * gate_sig).astype(jnp.bfloat16)
    past_rim = from_behind(glu[tok_rows - (kernel_len - 1) :], ("seq", "fsdp"), 1)
    padded_glu = jnp.concatenate([past_rim, glu], axis=0).astype(jnp.float32)
    conv_out = jnp.zeros((tok_rows, features), jnp.float32)
    for offset in range(kernel_len):
        conv_out = (
            conv_out
            + dw_kernel[offset]
            * padded_glu[kernel_len - 1 - offset : kernel_len - 1 - offset + tok_rows]
        )
    chan_mean, chan_var = mean_and_var(conv_out, ("fsdp", "seq"))
    conv_centred = conv_out - chan_mean
    bn_rstd = lax.rsqrt(chan_var + epsilon)
    chat = conv_centred * bn_rstd
    z_value = chat * bn_gain + bn_bias
    z_sig = jax.nn.sigmoid(z_value)
    output = (z_value * z_sig).astype(jnp.bfloat16)
    grad_z = cotangent.astype(jnp.float32) * z_sig * (1.0 + z_value * (1.0 - z_sig))
    grad_bn_bias, grad_bn_gain = fast_sum(
        (jnp.sum(grad_z, axis=0), jnp.sum(grad_z * chat, axis=0)), ("fsdp", "seq")
    )
    grad_conv = (
        bn_gain * bn_rstd * (grad_z - grad_bn_bias / all_frames - chat * grad_bn_gain / all_frames)
    )
    future_rim = from_behind(grad_conv[: kernel_len - 1], ("seq", "fsdp"), -1)
    padded_grad = jnp.concatenate([grad_conv, future_rim], axis=0)
    grad_glu = jnp.zeros((tok_rows, features), jnp.float32)
    kernel_rows = []
    for offset in range(kernel_len):
        grad_glu = grad_glu + dw_kernel[offset] * padded_grad[offset : offset + tok_rows]
        kernel_rows.append(
            jnp.sum(
                grad_conv
                * padded_glu[kernel_len - 1 - offset : kernel_len - 1 - offset + tok_rows],
                axis=0,
            )
        )
    kernel_portion = jnp.stack(kernel_rows, axis=0)
    grad_value = grad_glu * gate_sig
    grad_gate = grad_glu * value_part * gate_sig * (1.0 - gate_sig)
    grad_hidden = jnp.concatenate([grad_value, grad_gate], axis=1).astype(jnp.bfloat16)
    normalized_gradient = lax.dot_general(
        grad_hidden, full_weight, (((1,), (1,)), ((), ())), preferred_element_type=jnp.float32
    )
    rescaled_rows = normalized_gradient * layer_norm_gain
    input_gradient = row_inverse_deviation * (
        rescaled_rows
        - jnp.mean(rescaled_rows, axis=-1, keepdims=True)
        - standardized_input * jnp.mean(rescaled_rows * standardized_input, axis=-1, keepdims=True)
    )
    local_sums = (
        kernel_portion,
        jnp.sum(normalized_gradient * standardized_input, axis=0),
        jnp.sum(normalized_gradient, axis=0),
    )
    feature_rows = w_in.shape[0]
    group_rows = gather_own_columns(normalized_rows, "fsdp", feature_rows)
    contract = (((0,), (0,)), ((), ()))
    if lax.axis_size("fsdp") == 4:
        far = lax.ppermute(grad_hidden, "fsdp", [(i, i ^ 2) for i in range(4)])
        near = lax.ppermute(grad_hidden, "fsdp", [(i, i ^ 1) for i in range(4)])
        far, input_gradient, local_sums = lax.optimization_barrier(
            (far, input_gradient, local_sums)
        )
        near_far = lax.ppermute(far, "fsdp", [(i, i ^ 1) for i in range(4)])
        pieces = (grad_hidden, far, near, near_far)
        row_share = None
        for slot, piece in enumerate(pieces):
            term = lax.dot_general(
                group_rows[slot * tok_rows : (slot + 1) * tok_rows],
                piece,
                contract,
                preferred_element_type=jnp.float32,
            )
            row_share = term if row_share is None else row_share + term
    else:
        group_grad = lax.all_gather(grad_hidden, "fsdp", axis=0, tiled=True)
        row_share = lax.dot_general(
            group_rows, group_grad, contract, preferred_element_type=jnp.float32
        )
    reduced = lax.psum_scatter(row_share, "seq", scatter_dimension=0, tiled=True)
    grad_w_in = lax.all_gather(
        reduced.astype(jnp.bfloat16), "seq", axis=0, tiled=True
    ).astype(jnp.float32)
    grad_kernel, layer_norm_gain_gradient, grad_ln_bias = tree_sum(local_sums, ("seq", "fsdp"))
    return (
        output,
        input_gradient.astype(jnp.bfloat16),
        grad_w_in,
        grad_kernel,
        grad_bn_gain,
        grad_bn_bias,
        layer_norm_gain_gradient,
        grad_ln_bias,
    )


def solution(mesh):
    placed = (
        P(("seq", "fsdp"), None),
        P(),
        P(),
        P("fsdp", None),
        P(),
        P(),
        P(),
        P(("seq", "fsdp"), None),
    )
    return jax.shard_map(
        on_device,
        mesh=mesh,
        in_specs=placed,
        out_specs=(
            P(("seq", "fsdp"), None),
            P(("seq", "fsdp"), None),
            P("fsdp", None),
            P(),
            P(),
            P(),
            P(),
            P(),
        ),
        check_vma=False,
    )
```

```python
import jax
import jax.numpy as jnp
from jax import lax
from jax.sharding import PartitionSpec as P

epsilon = 1e-05


def from_behind(block, axis, distance):
    devices = range(lax.axis_size(axis))
    route = [(i - distance, i) for i in devices if i - distance in devices]
    return lax.ppermute(block, axis, route)


def tree_sum(tree, axis):
    count = lax.axis_size(axis)
    if count & (count - 1):
        return lax.psum(tree, axis)
    leaves, treedef = jax.tree.flatten(tree)
    width = leaves[0].shape[-1]
    packed = jnp.concatenate([leaf.reshape(-1, width) for leaf in leaves], axis=0)
    stride = 1
    while stride < count:
        route = [(i, i ^ stride) for i in range(count)]
        packed = packed + lax.ppermute(packed, axis, route)
        stride *= 2
    out, start = [], 0
    for leaf in leaves:
        rows = leaf.size // width
        out.append(packed[start : start + rows].reshape(leaf.shape))
        start += rows
    return jax.tree.unflatten(treedef, out)


def mean_and_var(block, axis):
    count = lax.axis_size(axis)
    frames = block.shape[0]
    if count & (count - 1):
        total = count * frames
        mean = lax.psum(jnp.sum(block, axis=0), axis) / total
        centred = block - mean
        return mean, lax.psum(jnp.sum(centred * centred, axis=0), axis) / total
    mean = jnp.mean(block, axis=0)
    centred = block - mean
    spread = jnp.sum(centred * centred, axis=0)
    stats = jnp.stack([mean, spread])
    rows, stride = frames, 1
    while stride < count:
        other = lax.ppermute(stats, axis, [(i, i ^ stride) for i in range(count)])
        delta = stats[0] - other[0]
        stats = jnp.stack(
            [
                (stats[0] + other[0]) * 0.5,
                (stats[1] + other[1]) + (0.5 * rows) * (delta * delta),
            ]
        )
        rows, stride = rows * 2, stride * 2
    return stats[0], stats[1] / rows


def group_shards(block, axis):
    far = lax.ppermute(block, axis, [(i, i ^ 2) for i in range(4)])
    near = lax.ppermute(block, axis, [(i, i ^ 1) for i in range(4)])
    near_far = lax.ppermute(far, axis, [(i, i ^ 1) for i in range(4)])
    return [block, far, near, near_far]


def gather_rows(block, axis):
    count = lax.axis_size(axis)
    if count != 4:
        return lax.all_gather(block, axis, axis=0, tiled=True)
    rows = block.shape[0]
    me = lax.axis_index(axis)
    shards = group_shards(block, axis)
    whole = jnp.zeros((count * rows,) + block.shape[1:], block.dtype)
    for shard, owner in zip(shards, (me, me ^ 2, me ^ 1, me ^ 3)):
        whole = lax.dynamic_update_slice_in_dim(whole, shard, owner * rows, axis=0)
    return whole


def gather_own_columns(rows_block, axis, width):
    me = lax.axis_index(axis)
    frames = rows_block.shape[0]

    def cols(owner):
        return lax.dynamic_slice_in_dim(rows_block, owner * width, width, axis=1)

    if lax.axis_size(axis) != 4:
        return lax.dynamic_slice_in_dim(
            lax.all_gather(rows_block, axis, axis=0, tiled=True), me * width, width, axis=1
        )
    far = lax.ppermute(
        jnp.concatenate([cols(me ^ 2), cols(me ^ 3)], axis=0), axis, [(i, i ^ 2) for i in range(4)]
    )
    near = lax.ppermute(
        jnp.concatenate([cols(me ^ 1), far[frames:]], axis=0), axis, [(i, i ^ 1) for i in range(4)]
    )
    return jnp.concatenate([cols(me), far[:frames], near], axis=0)


def on_device(
    inputs, layer_norm_gain, layer_norm_bias, w_in, dw_kernel, bn_gain, bn_bias, cotangent
):
    tok_rows = inputs.shape[0]
    features = inputs.shape[1]
    kernel_len = dw_kernel.shape[0]
    all_frames = tok_rows * lax.axis_size("seq") * lax.axis_size("fsdp")
    frames = inputs.astype(jnp.float32)
    row_mean = jnp.mean(frames, axis=-1, keepdims=True)
    centered_rows = frames - row_mean
    row_inverse_deviation = lax.rsqrt(
        jnp.mean(centered_rows * centered_rows, axis=-1, keepdims=True) + epsilon
    )
    standardized_input = centered_rows * row_inverse_deviation
    normalized_rows = (standardized_input * layer_norm_gain + layer_norm_bias).astype(jnp.bfloat16)
    full_weight = gather_rows(w_in, "fsdp")
    hidden = jnp.dot(normalized_rows, full_weight, preferred_element_type=jnp.float32)
    value_part = hidden[:, :features]
    gate_sig = jax.nn.sigmoid(hidden[:, features:])
    glu = (value_part * gate_sig).astype(jnp.bfloat16)
    past_rim = from_behind(glu[tok_rows - (kernel_len - 1) :], ("seq", "fsdp"), 1)
    padded_glu = jnp.concatenate([past_rim, glu], axis=0).astype(jnp.float32)
    conv_out = jnp.zeros((tok_rows, features), jnp.float32)
    for offset in range(kernel_len):
        conv_out = (
            conv_out
            + dw_kernel[offset]
            * padded_glu[kernel_len - 1 - offset : kernel_len - 1 - offset + tok_rows]
        )
    chan_mean, chan_var = mean_and_var(conv_out, ("seq", "fsdp"))
    conv_centred = conv_out - chan_mean
    bn_rstd = lax.rsqrt(chan_var + epsilon)
    chat = conv_centred * bn_rstd
    z_value = chat * bn_gain + bn_bias
    z_sig = jax.nn.sigmoid(z_value)
    output = (z_value * z_sig).astype(jnp.bfloat16)
    grad_z = cotangent.astype(jnp.float32) * z_sig * (1.0 + z_value * (1.0 - z_sig))
    grad_bn_bias, grad_bn_gain = tree_sum(
        (jnp.sum(grad_z, axis=0), jnp.sum(grad_z * chat, axis=0)), ("seq", "fsdp")
    )
    grad_conv = (
        bn_gain * bn_rstd * (grad_z - grad_bn_bias / all_frames - chat * grad_bn_gain / all_frames)
    )
    future_rim = from_behind(grad_conv[: kernel_len - 1], ("seq", "fsdp"), -1)
    padded_grad = jnp.concatenate([grad_conv, future_rim], axis=0)
    kernel_rows = []
    for offset in range(kernel_len):
        kernel_rows.append(
            jnp.sum(
                grad_conv
                * padded_glu[kernel_len - 1 - offset : kernel_len - 1 - offset + tok_rows],
                axis=0,
            )
        )
    kernel_portion = jnp.stack(kernel_rows, axis=0)
    half = tok_rows // 2
    spans = ((0, half), (half, tok_rows))
    gh_parts = []
    for lo, hi in spans:
        grad_glu = jnp.zeros((hi - lo, features), jnp.float32)
        for offset in range(kernel_len):
            grad_glu = grad_glu + dw_kernel[offset] * padded_grad[lo + offset : hi + offset]
        gate_rows = gate_sig[lo:hi]
        grad_value = grad_glu * gate_rows
        grad_gate = grad_glu * value_part[lo:hi] * gate_rows * (1.0 - gate_rows)
        gh_parts.append(jnp.concatenate([grad_value, grad_gate], axis=1).astype(jnp.bfloat16))
    grad_hidden = jnp.concatenate(gh_parts, axis=0)
    normalized_gradient = lax.dot_general(
        grad_hidden, full_weight, (((1,), (1,)), ((), ())), preferred_element_type=jnp.float32
    )
    rescaled_rows = normalized_gradient * layer_norm_gain
    input_gradient = row_inverse_deviation * (
        rescaled_rows
        - jnp.mean(rescaled_rows, axis=-1, keepdims=True)
        - standardized_input * jnp.mean(rescaled_rows * standardized_input, axis=-1, keepdims=True)
    )
    local_sums = (
        kernel_portion,
        jnp.sum(normalized_gradient * standardized_input, axis=0),
        jnp.sum(normalized_gradient, axis=0),
    )
    feature_rows = w_in.shape[0]
    group_rows = gather_own_columns(normalized_rows, "fsdp", feature_rows)
    contract = (((0,), (0,)), ((), ()))
    if lax.axis_size("fsdp") == 4:
        cross = [(i, i ^ 2) for i in range(4)]
        on_chip = [(i, i ^ 1) for i in range(4)]
        fars = [lax.ppermute(part, "fsdp", cross) for part in gh_parts]
        nears = [lax.ppermute(part, "fsdp", on_chip) for part in gh_parts]
        last_far, input_gradient, local_sums = lax.optimization_barrier(
            (fars[-1], input_gradient, local_sums)
        )
        fars[-1] = last_far
        near_fars = [lax.ppermute(far, "fsdp", on_chip) for far in fars]
        row_share = None
        for slot, parts in enumerate((gh_parts, fars, nears, near_fars)):
            for (lo, hi), piece in zip(spans, parts):
                term = lax.dot_general(
                    group_rows[slot * tok_rows + lo : slot * tok_rows + hi],
                    piece,
                    contract,
                    preferred_element_type=jnp.float32,
                )
                row_share = term if row_share is None else row_share + term
    else:
        group_grad = lax.all_gather(grad_hidden, "fsdp", axis=0, tiled=True)
        row_share = lax.dot_general(
            group_rows, group_grad, contract, preferred_element_type=jnp.float32
        )
    reduced = lax.psum_scatter(row_share, "seq", scatter_dimension=0, tiled=True)
    grad_w_in = lax.all_gather(
        reduced.astype(jnp.bfloat16), "seq", axis=0, tiled=True
    ).astype(jnp.float32)
    grad_kernel, layer_norm_gain_gradient, grad_ln_bias = tree_sum(local_sums, ("seq", "fsdp"))
    return (
        output,
        input_gradient.astype(jnp.bfloat16),
        grad_w_in,
        grad_kernel,
        grad_bn_gain,
        grad_bn_bias,
        layer_norm_gain_gradient,
        grad_ln_bias,
    )


def solution(mesh):
    placed = (
        P(("seq", "fsdp"), None),
        P(),
        P(),
        P("fsdp", None),
        P(),
        P(),
        P(),
        P(("seq", "fsdp"), None),
    )
    return jax.shard_map(
        on_device,
        mesh=mesh,
        in_specs=placed,
        out_specs=(
            P(("seq", "fsdp"), None),
            P(("seq", "fsdp"), None),
            P("fsdp", None),
            P(),
            P(),
            P(),
            P(),
            P(),
        ),
        check_vma=False,
    )
```

```python
import jax
import jax.numpy as jnp
from jax import lax
from jax.sharding import PartitionSpec as P

epsilon = 1e-05


def from_behind(block, axis, distance):
    devices = range(lax.axis_size(axis))
    route = [(i - distance, i) for i in devices if i - distance in devices]
    return lax.ppermute(block, axis, route)


def tree_sum(tree, axis):
    count = lax.axis_size(axis)
    if count & (count - 1):
        return lax.psum(tree, axis)
    leaves, treedef = jax.tree.flatten(tree)
    width = leaves[0].shape[-1]
    packed = jnp.concatenate([leaf.reshape(-1, width) for leaf in leaves], axis=0)
    stride = 1
    while stride < count:
        route = [(i, i ^ stride) for i in range(count)]
        packed = packed + lax.ppermute(packed, axis, route)
        stride *= 2
    out, start = [], 0
    for leaf in leaves:
        rows = leaf.size // width
        out.append(packed[start : start + rows].reshape(leaf.shape))
        start += rows
    return jax.tree.unflatten(treedef, out)


def mean_and_var(block, axis):
    count = lax.axis_size(axis)
    frames = block.shape[0]
    if count & (count - 1):
        total = count * frames
        mean = lax.psum(jnp.sum(block, axis=0), axis) / total
        centred = block - mean
        return mean, lax.psum(jnp.sum(centred * centred, axis=0), axis) / total
    mean = jnp.mean(block, axis=0)
    centred = block - mean
    spread = jnp.sum(centred * centred, axis=0)
    stats = jnp.stack([mean, spread])
    rows, stride = frames, 1
    while stride < count:
        other = lax.ppermute(stats, axis, [(i, i ^ stride) for i in range(count)])
        delta = stats[0] - other[0]
        stats = jnp.stack(
            [
                (stats[0] + other[0]) * 0.5,
                (stats[1] + other[1]) + (0.5 * rows) * (delta * delta),
            ]
        )
        rows, stride = rows * 2, stride * 2
    return stats[0], stats[1] / rows


def group_shards(block, axis):
    far = lax.ppermute(block, axis, [(i, i ^ 2) for i in range(4)])
    near = lax.ppermute(block, axis, [(i, i ^ 1) for i in range(4)])
    near_far = lax.ppermute(far, axis, [(i, i ^ 1) for i in range(4)])
    return [block, far, near, near_far]


def gather_rows(block, axis):
    count = lax.axis_size(axis)
    if count != 4:
        return lax.all_gather(block, axis, axis=0, tiled=True)
    rows = block.shape[0]
    me = lax.axis_index(axis)
    shards = group_shards(block, axis)
    whole = jnp.zeros((count * rows,) + block.shape[1:], block.dtype)
    for shard, owner in zip(shards, (me, me ^ 2, me ^ 1, me ^ 3)):
        whole = lax.dynamic_update_slice_in_dim(whole, shard, owner * rows, axis=0)
    return whole


def gather_weight(block, axis, twin):
    if lax.axis_size(axis) != 4 or lax.axis_size(twin) % 2 or block.shape[1] % 512:
        return gather_rows(block, axis)
    rows, width = block.shape
    piece = width // 4
    bit = lax.axis_index(twin) % 2
    cross = [(i, i ^ 2) for i in range(4)]
    on_chip = [(i, i ^ 1) for i in range(4)]
    pairs = [(i, i ^ 1) for i in range(lax.axis_size(twin))]
    near = lax.ppermute(block, axis, on_chip)
    first = lax.ppermute(
        lax.dynamic_slice_in_dim(block, bit * piece, piece, axis=1), axis, cross
    )
    second_out, first = lax.optimization_barrier(
        (lax.dynamic_slice_in_dim(block, (bit + 2) * piece, piece, axis=1), first)
    )
    second = lax.ppermute(second_out, axis, cross)
    first_twin = lax.ppermute(first, twin, pairs)
    second_twin = lax.ppermute(second, twin, pairs)
    low = bit == 0
    far = jnp.concatenate(
        [
            jnp.where(low, first, first_twin),
            jnp.where(low, first_twin, first),
            jnp.where(low, second, second_twin),
            jnp.where(low, second_twin, second),
        ],
        axis=1,
    )
    near_far = lax.ppermute(far, axis, on_chip)
    me = lax.axis_index(axis)
    whole = jnp.zeros((4 * rows, width), block.dtype)
    for shard, owner in zip((block, far, near, near_far), (me, me ^ 2, me ^ 1, me ^ 3)):
        whole = lax.dynamic_update_slice_in_dim(whole, shard, owner * rows, axis=0)
    return whole


def gather_own_columns(rows_block, axis, width):
    me = lax.axis_index(axis)
    frames = rows_block.shape[0]

    def cols(owner):
        return lax.dynamic_slice_in_dim(rows_block, owner * width, width, axis=1)

    if lax.axis_size(axis) != 4:
        return lax.dynamic_slice_in_dim(
            lax.all_gather(rows_block, axis, axis=0, tiled=True), me * width, width, axis=1
        )
    far = lax.ppermute(
        jnp.concatenate([cols(me ^ 2), cols(me ^ 3)], axis=0), axis, [(i, i ^ 2) for i in range(4)]
    )
    near = lax.ppermute(
        jnp.concatenate([cols(me ^ 1), far[frames:]], axis=0), axis, [(i, i ^ 1) for i in range(4)]
    )
    return jnp.concatenate([cols(me), far[:frames], near], axis=0)


def on_device(
    inputs, layer_norm_gain, layer_norm_bias, w_in, dw_kernel, bn_gain, bn_bias, cotangent
):
    tok_rows = inputs.shape[0]
    features = inputs.shape[1]
    kernel_len = dw_kernel.shape[0]
    all_frames = tok_rows * lax.axis_size("seq") * lax.axis_size("fsdp")
    frames = inputs.astype(jnp.float32)
    row_mean = jnp.mean(frames, axis=-1, keepdims=True)
    centered_rows = frames - row_mean
    row_inverse_deviation = lax.rsqrt(
        jnp.mean(centered_rows * centered_rows, axis=-1, keepdims=True) + epsilon
    )
    standardized_input = centered_rows * row_inverse_deviation
    normalized_rows = (standardized_input * layer_norm_gain + layer_norm_bias).astype(jnp.bfloat16)
    full_weight = gather_weight(w_in, "fsdp", "seq")
    hidden = jnp.dot(normalized_rows, full_weight, preferred_element_type=jnp.float32)
    value_part = hidden[:, :features]
    gate_sig = jax.nn.sigmoid(hidden[:, features:])
    glu = (value_part * gate_sig).astype(jnp.bfloat16)
    past_rim = from_behind(glu[tok_rows - (kernel_len - 1) :], ("seq", "fsdp"), 1)
    padded_glu = jnp.concatenate([past_rim, glu], axis=0).astype(jnp.float32)
    conv_out = jnp.zeros((tok_rows, features), jnp.float32)
    for offset in range(kernel_len):
        conv_out = (
            conv_out
            + dw_kernel[offset]
            * padded_glu[kernel_len - 1 - offset : kernel_len - 1 - offset + tok_rows]
        )
    chan_mean, chan_var = mean_and_var(conv_out, ("seq", "fsdp"))
    conv_centred = conv_out - chan_mean
    bn_rstd = lax.rsqrt(chan_var + epsilon)
    chat = conv_centred * bn_rstd
    z_value = chat * bn_gain + bn_bias
    z_sig = jax.nn.sigmoid(z_value)
    output = (z_value * z_sig).astype(jnp.bfloat16)
    grad_z = cotangent.astype(jnp.float32) * z_sig * (1.0 + z_value * (1.0 - z_sig))
    grad_bn_bias, grad_bn_gain = tree_sum(
        (jnp.sum(grad_z, axis=0), jnp.sum(grad_z * chat, axis=0)), ("seq", "fsdp")
    )
    grad_conv = (
        bn_gain * bn_rstd * (grad_z - grad_bn_bias / all_frames - chat * grad_bn_gain / all_frames)
    )
    future_rim = from_behind(grad_conv[: kernel_len - 1], ("seq", "fsdp"), -1)
    padded_grad = jnp.concatenate([grad_conv, future_rim], axis=0)
    grad_glu = jnp.zeros((tok_rows, features), jnp.float32)
    kernel_rows = []
    for offset in range(kernel_len):
        grad_glu = grad_glu + dw_kernel[offset] * padded_grad[offset : offset + tok_rows]
        kernel_rows.append(
            jnp.sum(
                grad_conv
                * padded_glu[kernel_len - 1 - offset : kernel_len - 1 - offset + tok_rows],
                axis=0,
            )
        )
    kernel_portion = jnp.stack(kernel_rows, axis=0)
    grad_value = grad_glu * gate_sig
    grad_gate = grad_glu * value_part * gate_sig * (1.0 - gate_sig)
    grad_hidden = jnp.concatenate([grad_value, grad_gate], axis=1).astype(jnp.bfloat16)
    normalized_gradient = lax.dot_general(
        grad_hidden, full_weight, (((1,), (1,)), ((), ())), preferred_element_type=jnp.float32
    )
    rescaled_rows = normalized_gradient * layer_norm_gain
    input_gradient = row_inverse_deviation * (
        rescaled_rows
        - jnp.mean(rescaled_rows, axis=-1, keepdims=True)
        - standardized_input * jnp.mean(rescaled_rows * standardized_input, axis=-1, keepdims=True)
    )
    local_sums = (
        kernel_portion,
        jnp.sum(normalized_gradient * standardized_input, axis=0),
        jnp.sum(normalized_gradient, axis=0),
    )
    feature_rows = w_in.shape[0]
    group_rows = gather_own_columns(normalized_rows, "fsdp", feature_rows)
    contract = (((0,), (0,)), ((), ()))
    if lax.axis_size("fsdp") == 4:
        far = lax.ppermute(grad_hidden, "fsdp", [(i, i ^ 2) for i in range(4)])
        near = lax.ppermute(grad_hidden, "fsdp", [(i, i ^ 1) for i in range(4)])
        far, input_gradient, local_sums = lax.optimization_barrier(
            (far, input_gradient, local_sums)
        )
        near_far = lax.ppermute(far, "fsdp", [(i, i ^ 1) for i in range(4)])
        pieces = (grad_hidden, far, near, near_far)
        row_share = None
        for slot, piece in enumerate(pieces):
            term = lax.dot_general(
                group_rows[slot * tok_rows : (slot + 1) * tok_rows],
                piece,
                contract,
                preferred_element_type=jnp.float32,
            )
            row_share = term if row_share is None else row_share + term
    else:
        group_grad = lax.all_gather(grad_hidden, "fsdp", axis=0, tiled=True)
        row_share = lax.dot_general(
            group_rows, group_grad, contract, preferred_element_type=jnp.float32
        )
    reduced = lax.psum_scatter(row_share, "seq", scatter_dimension=0, tiled=True)
    grad_w_in = lax.all_gather(
        reduced.astype(jnp.bfloat16), "seq", axis=0, tiled=True
    ).astype(jnp.float32)
    grad_kernel, layer_norm_gain_gradient, grad_ln_bias = tree_sum(local_sums, ("seq", "fsdp"))
    return (
        output,
        input_gradient.astype(jnp.bfloat16),
        grad_w_in,
        grad_kernel,
        grad_bn_gain,
        grad_bn_bias,
        layer_norm_gain_gradient,
        grad_ln_bias,
    )


def solution(mesh):
    placed = (
        P(("seq", "fsdp"), None),
        P(),
        P(),
        P("fsdp", None),
        P(),
        P(),
        P(),
        P(("seq", "fsdp"), None),
    )
    return jax.shard_map(
        on_device,
        mesh=mesh,
        in_specs=placed,
        out_specs=(
            P(("seq", "fsdp"), None),
            P(("seq", "fsdp"), None),
            P("fsdp", None),
            P(),
            P(),
            P(),
            P(),
            P(),
        ),
        check_vma=False,
    )
```

```python
import jax
import jax.numpy as jnp
from jax import lax
from jax.sharding import PartitionSpec as P

epsilon = 1e-05


def from_behind(block, axis, distance):
    devices = range(lax.axis_size(axis))
    route = [(i - distance, i) for i in devices if i - distance in devices]
    return lax.ppermute(block, axis, route)


def tree_sum(tree, axis):
    count = lax.axis_size(axis)
    if count & (count - 1):
        return lax.psum(tree, axis)
    leaves, treedef = jax.tree.flatten(tree)
    width = leaves[0].shape[-1]
    packed = jnp.concatenate([leaf.reshape(-1, width) for leaf in leaves], axis=0)
    stride = 1
    while stride < count:
        route = [(i, i ^ stride) for i in range(count)]
        packed = packed + lax.ppermute(packed, axis, route)
        stride *= 2
    out, start = [], 0
    for leaf in leaves:
        rows = leaf.size // width
        out.append(packed[start : start + rows].reshape(leaf.shape))
        start += rows
    return jax.tree.unflatten(treedef, out)


def mean_and_var(block, axis):
    count = lax.axis_size(axis)
    frames = block.shape[0]
    if count & (count - 1):
        total = count * frames
        mean = lax.psum(jnp.sum(block, axis=0), axis) / total
        centred = block - mean
        return mean, lax.psum(jnp.sum(centred * centred, axis=0), axis) / total
    mean = jnp.mean(block, axis=0)
    centred = block - mean
    spread = jnp.sum(centred * centred, axis=0)
    stats = jnp.stack([mean, spread])
    rows, stride = frames, 1
    while stride < count:
        other = lax.ppermute(stats, axis, [(i, i ^ stride) for i in range(count)])
        delta = stats[0] - other[0]
        stats = jnp.stack(
            [
                (stats[0] + other[0]) * 0.5,
                (stats[1] + other[1]) + (0.5 * rows) * (delta * delta),
            ]
        )
        rows, stride = rows * 2, stride * 2
    return stats[0], stats[1] / rows


def group_shards(block, axis):
    far = lax.ppermute(block, axis, [(i, i ^ 2) for i in range(4)])
    near = lax.ppermute(block, axis, [(i, i ^ 1) for i in range(4)])
    near_far = lax.ppermute(far, axis, [(i, i ^ 1) for i in range(4)])
    return [block, far, near, near_far]


def gather_rows(block, axis):
    count = lax.axis_size(axis)
    if count != 4:
        return lax.all_gather(block, axis, axis=0, tiled=True)
    rows = block.shape[0]
    me = lax.axis_index(axis)
    shards = group_shards(block, axis)
    whole = jnp.zeros((count * rows,) + block.shape[1:], block.dtype)
    for shard, owner in zip(shards, (me, me ^ 2, me ^ 1, me ^ 3)):
        whole = lax.dynamic_update_slice_in_dim(whole, shard, owner * rows, axis=0)
    return whole


def gather_own_columns(rows_block, axis, width):
    me = lax.axis_index(axis)
    frames = rows_block.shape[0]

    def cols(owner):
        return lax.dynamic_slice_in_dim(rows_block, owner * width, width, axis=1)

    if lax.axis_size(axis) != 4:
        return lax.dynamic_slice_in_dim(
            lax.all_gather(rows_block, axis, axis=0, tiled=True), me * width, width, axis=1
        )
    far = lax.ppermute(
        jnp.concatenate([cols(me ^ 2), cols(me ^ 3)], axis=0), axis, [(i, i ^ 2) for i in range(4)]
    )
    near = lax.ppermute(
        jnp.concatenate([cols(me ^ 1), far[frames:]], axis=0), axis, [(i, i ^ 1) for i in range(4)]
    )
    return jnp.concatenate([cols(me), far[:frames], near], axis=0)


def on_device(
    inputs, layer_norm_gain, layer_norm_bias, w_in, dw_kernel, bn_gain, bn_bias, cotangent
):
    tok_rows = inputs.shape[0]
    features = inputs.shape[1]
    kernel_len = dw_kernel.shape[0]
    all_frames = tok_rows * lax.axis_size("seq") * lax.axis_size("fsdp")
    frames = inputs.astype(jnp.float32)
    row_mean = jnp.mean(frames, axis=-1, keepdims=True)
    centered_rows = frames - row_mean
    row_inverse_deviation = lax.rsqrt(
        jnp.mean(centered_rows * centered_rows, axis=-1, keepdims=True) + epsilon
    )
    standardized_input = centered_rows * row_inverse_deviation
    normalized_rows = (standardized_input * layer_norm_gain + layer_norm_bias).astype(jnp.bfloat16)
    if lax.axis_size("fsdp") == 4:
        weight_rows = w_in.shape[0]
        me = lax.axis_index("fsdp")
        shards = group_shards(w_in, "fsdp")
        owners = (me, me ^ 2, me ^ 1, me ^ 3)
        hidden = None
        for shard, owner in zip(shards, owners):
            term = jnp.dot(
                lax.dynamic_slice_in_dim(normalized_rows, owner * weight_rows, weight_rows, axis=1),
                shard,
                preferred_element_type=jnp.float32,
            )
            hidden = term if hidden is None else hidden + term
        full_weight = jnp.zeros((4 * weight_rows, w_in.shape[1]), w_in.dtype)
        for shard, owner in zip(shards, owners):
            full_weight = lax.dynamic_update_slice_in_dim(
                full_weight, shard, owner * weight_rows, axis=0
            )
    else:
        full_weight = lax.all_gather(w_in, "fsdp", axis=0, tiled=True)
        hidden = jnp.dot(normalized_rows, full_weight, preferred_element_type=jnp.float32)
    value_part = hidden[:, :features]
    gate_sig = jax.nn.sigmoid(hidden[:, features:])
    glu = (value_part * gate_sig).astype(jnp.bfloat16)
    past_rim = from_behind(glu[tok_rows - (kernel_len - 1) :], ("seq", "fsdp"), 1)
    padded_glu = jnp.concatenate([past_rim, glu], axis=0).astype(jnp.float32)
    conv_out = jnp.zeros((tok_rows, features), jnp.float32)
    for offset in range(kernel_len):
        conv_out = (
            conv_out
            + dw_kernel[offset]
            * padded_glu[kernel_len - 1 - offset : kernel_len - 1 - offset + tok_rows]
        )
    chan_mean, chan_var = mean_and_var(conv_out, ("seq", "fsdp"))
    conv_centred = conv_out - chan_mean
    bn_rstd = lax.rsqrt(chan_var + epsilon)
    chat = conv_centred * bn_rstd
    z_value = chat * bn_gain + bn_bias
    z_sig = jax.nn.sigmoid(z_value)
    output = (z_value * z_sig).astype(jnp.bfloat16)
    grad_z = cotangent.astype(jnp.float32) * z_sig * (1.0 + z_value * (1.0 - z_sig))
    grad_bn_bias, grad_bn_gain = tree_sum(
        (jnp.sum(grad_z, axis=0), jnp.sum(grad_z * chat, axis=0)), ("seq", "fsdp")
    )
    grad_conv = (
        bn_gain * bn_rstd * (grad_z - grad_bn_bias / all_frames - chat * grad_bn_gain / all_frames)
    )
    future_rim = from_behind(grad_conv[: kernel_len - 1], ("seq", "fsdp"), -1)
    padded_grad = jnp.concatenate([grad_conv, future_rim], axis=0)
    grad_glu = jnp.zeros((tok_rows, features), jnp.float32)
    kernel_rows = []
    for offset in range(kernel_len):
        grad_glu = grad_glu + dw_kernel[offset] * padded_grad[offset : offset + tok_rows]
        kernel_rows.append(
            jnp.sum(
                grad_conv
                * padded_glu[kernel_len - 1 - offset : kernel_len - 1 - offset + tok_rows],
                axis=0,
            )
        )
    kernel_portion = jnp.stack(kernel_rows, axis=0)
    grad_value = grad_glu * gate_sig
    grad_gate = grad_glu * value_part * gate_sig * (1.0 - gate_sig)
    grad_hidden = jnp.concatenate([grad_value, grad_gate], axis=1).astype(jnp.bfloat16)
    normalized_gradient = lax.dot_general(
        grad_hidden, full_weight, (((1,), (1,)), ((), ())), preferred_element_type=jnp.float32
    )
    rescaled_rows = normalized_gradient * layer_norm_gain
    input_gradient = row_inverse_deviation * (
        rescaled_rows
        - jnp.mean(rescaled_rows, axis=-1, keepdims=True)
        - standardized_input * jnp.mean(rescaled_rows * standardized_input, axis=-1, keepdims=True)
    )
    local_sums = (
        kernel_portion,
        jnp.sum(normalized_gradient * standardized_input, axis=0),
        jnp.sum(normalized_gradient, axis=0),
    )
    feature_rows = w_in.shape[0]
    group_rows = gather_own_columns(normalized_rows, "fsdp", feature_rows)
    contract = (((0,), (0,)), ((), ()))
    if lax.axis_size("fsdp") == 4:
        far = lax.ppermute(grad_hidden, "fsdp", [(i, i ^ 2) for i in range(4)])
        near = lax.ppermute(grad_hidden, "fsdp", [(i, i ^ 1) for i in range(4)])
        far, input_gradient, local_sums = lax.optimization_barrier(
            (far, input_gradient, local_sums)
        )
        near_far = lax.ppermute(far, "fsdp", [(i, i ^ 1) for i in range(4)])
        pieces = (grad_hidden, far, near, near_far)
        row_share = None
        for slot, piece in enumerate(pieces):
            term = lax.dot_general(
                group_rows[slot * tok_rows : (slot + 1) * tok_rows],
                piece,
                contract,
                preferred_element_type=jnp.float32,
            )
            row_share = term if row_share is None else row_share + term
    else:
        group_grad = lax.all_gather(grad_hidden, "fsdp", axis=0, tiled=True)
        row_share = lax.dot_general(
            group_rows, group_grad, contract, preferred_element_type=jnp.float32
        )
    reduced = lax.psum_scatter(row_share, "seq", scatter_dimension=0, tiled=True)
    grad_w_in = lax.all_gather(
        reduced.astype(jnp.bfloat16), "seq", axis=0, tiled=True
    ).astype(jnp.float32)
    grad_kernel, layer_norm_gain_gradient, grad_ln_bias = tree_sum(local_sums, ("seq", "fsdp"))
    return (
        output,
        input_gradient.astype(jnp.bfloat16),
        grad_w_in,
        grad_kernel,
        grad_bn_gain,
        grad_bn_bias,
        layer_norm_gain_gradient,
        grad_ln_bias,
    )


def solution(mesh):
    placed = (
        P(("seq", "fsdp"), None),
        P(),
        P(),
        P("fsdp", None),
        P(),
        P(),
        P(),
        P(("seq", "fsdp"), None),
    )
    return jax.shard_map(
        on_device,
        mesh=mesh,
        in_specs=placed,
        out_specs=(
            P(("seq", "fsdp"), None),
            P(("seq", "fsdp"), None),
            P("fsdp", None),
            P(),
            P(),
            P(),
            P(),
            P(),
        ),
        check_vma=False,
    )
```

```python
import jax
import jax.numpy as jnp
from jax import lax
from jax.sharding import PartitionSpec as P

epsilon = 1e-05


def from_behind(block, axis, distance):
    devices = range(lax.axis_size(axis))
    route = [(i - distance, i) for i in devices if i - distance in devices]
    return lax.ppermute(block, axis, route)


def tree_sum(tree, axis):
    count = lax.axis_size(axis)
    if count & (count - 1):
        return lax.psum(tree, axis)
    leaves, treedef = jax.tree.flatten(tree)
    width = leaves[0].shape[-1]
    packed = jnp.concatenate([leaf.reshape(-1, width) for leaf in leaves], axis=0)
    stride = 1
    while stride < count:
        route = [(i, i ^ stride) for i in range(count)]
        packed = packed + lax.ppermute(packed, axis, route)
        stride *= 2
    out, start = [], 0
    for leaf in leaves:
        rows = leaf.size // width
        out.append(packed[start : start + rows].reshape(leaf.shape))
        start += rows
    return jax.tree.unflatten(treedef, out)


def mean_and_var(block, axis):
    count = lax.axis_size(axis)
    frames = block.shape[0]
    if count & (count - 1):
        total = count * frames
        mean = lax.psum(jnp.sum(block, axis=0), axis) / total
        centred = block - mean
        return mean, lax.psum(jnp.sum(centred * centred, axis=0), axis) / total
    mean = jnp.mean(block, axis=0)
    centred = block - mean
    spread = jnp.sum(centred * centred, axis=0)
    stats = jnp.stack([mean, spread])
    rows, stride = frames, 1
    while stride < count:
        other = lax.ppermute(stats, axis, [(i, i ^ stride) for i in range(count)])
        delta = stats[0] - other[0]
        stats = jnp.stack(
            [
                (stats[0] + other[0]) * 0.5,
                (stats[1] + other[1]) + (0.5 * rows) * (delta * delta),
            ]
        )
        rows, stride = rows * 2, stride * 2
    return stats[0], stats[1] / rows


def group_shards(block, axis, cover=None):
    far = lax.ppermute(block, axis, [(i, i ^ 2) for i in range(4)])
    if cover is not None:
        far, _ = lax.optimization_barrier((far, cover))
    near = lax.ppermute(block, axis, [(i, i ^ 1) for i in range(4)])
    near_far = lax.ppermute(far, axis, [(i, i ^ 1) for i in range(4)])
    return [block, far, near, near_far]


def gather_rows(block, axis, cover=None):
    count = lax.axis_size(axis)
    if count != 4:
        return lax.all_gather(block, axis, axis=0, tiled=True)
    rows = block.shape[0]
    me = lax.axis_index(axis)
    shards = group_shards(block, axis, cover)
    whole = jnp.zeros((count * rows,) + block.shape[1:], block.dtype)
    for shard, owner in zip(shards, (me, me ^ 2, me ^ 1, me ^ 3)):
        whole = lax.dynamic_update_slice_in_dim(whole, shard, owner * rows, axis=0)
    return whole


def gather_own_columns(rows_block, axis, width):
    me = lax.axis_index(axis)
    frames = rows_block.shape[0]

    def cols(owner):
        return lax.dynamic_slice_in_dim(rows_block, owner * width, width, axis=1)

    if lax.axis_size(axis) != 4:
        return lax.dynamic_slice_in_dim(
            lax.all_gather(rows_block, axis, axis=0, tiled=True), me * width, width, axis=1
        )
    far = lax.ppermute(
        jnp.concatenate([cols(me ^ 2), cols(me ^ 3)], axis=0), axis, [(i, i ^ 2) for i in range(4)]
    )
    near = lax.ppermute(
        jnp.concatenate([cols(me ^ 1), far[frames:]], axis=0), axis, [(i, i ^ 1) for i in range(4)]
    )
    return jnp.concatenate([cols(me), far[:frames], near], axis=0)


def on_device(
    inputs, layer_norm_gain, layer_norm_bias, w_in, dw_kernel, bn_gain, bn_bias, cotangent
):
    tok_rows = inputs.shape[0]
    features = inputs.shape[1]
    kernel_len = dw_kernel.shape[0]
    all_frames = tok_rows * lax.axis_size("seq") * lax.axis_size("fsdp")
    frames = inputs.astype(jnp.float32)
    row_mean = jnp.mean(frames, axis=-1, keepdims=True)
    centered_rows = frames - row_mean
    row_inverse_deviation = lax.rsqrt(
        jnp.mean(centered_rows * centered_rows, axis=-1, keepdims=True) + epsilon
    )
    standardized_input = centered_rows * row_inverse_deviation
    normalized_rows = (standardized_input * layer_norm_gain + layer_norm_bias).astype(jnp.bfloat16)
    full_weight = gather_rows(w_in, "fsdp", normalized_rows)
    hidden = jnp.dot(normalized_rows, full_weight, preferred_element_type=jnp.float32)
    value_part = hidden[:, :features]
    gate_sig = jax.nn.sigmoid(hidden[:, features:])
    glu = (value_part * gate_sig).astype(jnp.bfloat16)
    past_rim = from_behind(glu[tok_rows - (kernel_len - 1) :], ("seq", "fsdp"), 1)
    padded_glu = jnp.concatenate([past_rim, glu], axis=0).astype(jnp.float32)
    conv_out = jnp.zeros((tok_rows, features), jnp.float32)
    for offset in range(kernel_len):
        conv_out = (
            conv_out
            + dw_kernel[offset]
            * padded_glu[kernel_len - 1 - offset : kernel_len - 1 - offset + tok_rows]
        )
    chan_mean, chan_var = mean_and_var(conv_out, ("seq", "fsdp"))
    conv_centred = conv_out - chan_mean
    bn_rstd = lax.rsqrt(chan_var + epsilon)
    chat = conv_centred * bn_rstd
    z_value = chat * bn_gain + bn_bias
    z_sig = jax.nn.sigmoid(z_value)
    output = (z_value * z_sig).astype(jnp.bfloat16)
    grad_z = cotangent.astype(jnp.float32) * z_sig * (1.0 + z_value * (1.0 - z_sig))
    grad_bn_bias, grad_bn_gain = tree_sum(
        (jnp.sum(grad_z, axis=0), jnp.sum(grad_z * chat, axis=0)), ("seq", "fsdp")
    )
    grad_conv = (
        bn_gain * bn_rstd * (grad_z - grad_bn_bias / all_frames - chat * grad_bn_gain / all_frames)
    )
    future_rim = from_behind(grad_conv[: kernel_len - 1], ("seq", "fsdp"), -1)
    padded_grad = jnp.concatenate([grad_conv, future_rim], axis=0)
    grad_glu = jnp.zeros((tok_rows, features), jnp.float32)
    kernel_rows = []
    for offset in range(kernel_len):
        grad_glu = grad_glu + dw_kernel[offset] * padded_grad[offset : offset + tok_rows]
        kernel_rows.append(
            jnp.sum(
                grad_conv
                * padded_glu[kernel_len - 1 - offset : kernel_len - 1 - offset + tok_rows],
                axis=0,
            )
        )
    kernel_portion = jnp.stack(kernel_rows, axis=0)
    grad_value = grad_glu * gate_sig
    grad_gate = grad_glu * value_part * gate_sig * (1.0 - gate_sig)
    grad_hidden = jnp.concatenate([grad_value, grad_gate], axis=1).astype(jnp.bfloat16)
    normalized_gradient = lax.dot_general(
        grad_hidden, full_weight, (((1,), (1,)), ((), ())), preferred_element_type=jnp.float32
    )
    rescaled_rows = normalized_gradient * layer_norm_gain
    input_gradient = row_inverse_deviation * (
        rescaled_rows
        - jnp.mean(rescaled_rows, axis=-1, keepdims=True)
        - standardized_input * jnp.mean(rescaled_rows * standardized_input, axis=-1, keepdims=True)
    )
    local_sums = (
        kernel_portion,
        jnp.sum(normalized_gradient * standardized_input, axis=0),
        jnp.sum(normalized_gradient, axis=0),
    )
    feature_rows = w_in.shape[0]
    group_rows = gather_own_columns(normalized_rows, "fsdp", feature_rows)
    contract = (((0,), (0,)), ((), ()))
    if lax.axis_size("fsdp") == 4:
        far = lax.ppermute(grad_hidden, "fsdp", [(i, i ^ 2) for i in range(4)])
        near = lax.ppermute(grad_hidden, "fsdp", [(i, i ^ 1) for i in range(4)])
        far, input_gradient, local_sums = lax.optimization_barrier(
            (far, input_gradient, local_sums)
        )
        near_far = lax.ppermute(far, "fsdp", [(i, i ^ 1) for i in range(4)])
        pieces = (grad_hidden, far, near, near_far)
        row_share = None
        for slot, piece in enumerate(pieces):
            term = lax.dot_general(
                group_rows[slot * tok_rows : (slot + 1) * tok_rows],
                piece,
                contract,
                preferred_element_type=jnp.float32,
            )
            row_share = term if row_share is None else row_share + term
    else:
        group_grad = lax.all_gather(grad_hidden, "fsdp", axis=0, tiled=True)
        row_share = lax.dot_general(
            group_rows, group_grad, contract, preferred_element_type=jnp.float32
        )
    reduced = lax.psum_scatter(row_share, "seq", scatter_dimension=0, tiled=True)
    grad_w_in = lax.all_gather(
        reduced.astype(jnp.bfloat16), "seq", axis=0, tiled=True
    ).astype(jnp.float32)
    grad_kernel, layer_norm_gain_gradient, grad_ln_bias = tree_sum(local_sums, ("seq", "fsdp"))
    return (
        output,
        input_gradient.astype(jnp.bfloat16),
        grad_w_in,
        grad_kernel,
        grad_bn_gain,
        grad_bn_bias,
        layer_norm_gain_gradient,
        grad_ln_bias,
    )


def solution(mesh):
    placed = (
        P(("seq", "fsdp"), None),
        P(),
        P(),
        P("fsdp", None),
        P(),
        P(),
        P(),
        P(("seq", "fsdp"), None),
    )
    return jax.shard_map(
        on_device,
        mesh=mesh,
        in_specs=placed,
        out_specs=(
            P(("seq", "fsdp"), None),
            P(("seq", "fsdp"), None),
            P("fsdp", None),
            P(),
            P(),
            P(),
            P(),
            P(),
        ),
        check_vma=False,
    )
```

```python
import jax
import jax.numpy as jnp
from jax import lax
from jax.sharding import PartitionSpec as P

epsilon = 1e-05


def from_behind(block, axis, distance):
    devices = range(lax.axis_size(axis))
    route = [(i - distance, i) for i in devices if i - distance in devices]
    return lax.ppermute(block, axis, route)


def tree_sum(tree, axis):
    count = lax.axis_size(axis)
    if count & (count - 1):
        return lax.psum(tree, axis)
    leaves, treedef = jax.tree.flatten(tree)
    width = leaves[0].shape[-1]
    packed = jnp.concatenate([leaf.reshape(-1, width) for leaf in leaves], axis=0)
    stride = 1
    while stride < count:
        route = [(i, i ^ stride) for i in range(count)]
        packed = packed + lax.ppermute(packed, axis, route)
        stride *= 2
    out, start = [], 0
    for leaf in leaves:
        rows = leaf.size // width
        out.append(packed[start : start + rows].reshape(leaf.shape))
        start += rows
    return jax.tree.unflatten(treedef, out)


def mean_and_var(block, axis):
    count = lax.axis_size(axis)
    frames = block.shape[0]
    if count & (count - 1):
        total = count * frames
        mean = lax.psum(jnp.sum(block, axis=0), axis) / total
        centred = block - mean
        return mean, lax.psum(jnp.sum(centred * centred, axis=0), axis) / total
    mean = jnp.mean(block, axis=0)
    centred = block - mean
    spread = jnp.sum(centred * centred, axis=0)
    stats = jnp.stack([mean, spread])
    rows, stride = frames, 1
    while stride < count:
        other = lax.ppermute(stats, axis, [(i, i ^ stride) for i in range(count)])
        delta = stats[0] - other[0]
        stats = jnp.stack(
            [
                (stats[0] + other[0]) * 0.5,
                (stats[1] + other[1]) + (0.5 * rows) * (delta * delta),
            ]
        )
        rows, stride = rows * 2, stride * 2
    return stats[0], stats[1] / rows


def group_shards(block, axis):
    far = lax.ppermute(block, axis, [(i, i ^ 2) for i in range(4)])
    near = lax.ppermute(block, axis, [(i, i ^ 1) for i in range(4)])
    near_far = lax.ppermute(far, axis, [(i, i ^ 1) for i in range(4)])
    return [block, far, near, near_far]


def gather_rows(block, axis):
    count = lax.axis_size(axis)
    if count != 4:
        return lax.all_gather(block, axis, axis=0, tiled=True)
    rows = block.shape[0]
    me = lax.axis_index(axis)
    shards = group_shards(block, axis)
    whole = jnp.zeros((count * rows,) + block.shape[1:], block.dtype)
    for shard, owner in zip(shards, (me, me ^ 2, me ^ 1, me ^ 3)):
        whole = lax.dynamic_update_slice_in_dim(whole, shard, owner * rows, axis=0)
    return whole


def gather_own_columns(rows_block, axis, width):
    me = lax.axis_index(axis)
    frames = rows_block.shape[0]

    def cols(owner):
        return lax.dynamic_slice_in_dim(rows_block, owner * width, width, axis=1)

    if lax.axis_size(axis) != 4:
        return lax.dynamic_slice_in_dim(
            lax.all_gather(rows_block, axis, axis=0, tiled=True), me * width, width, axis=1
        )
    far = lax.ppermute(
        jnp.concatenate([cols(me ^ 2), cols(me ^ 3)], axis=0), axis, [(i, i ^ 2) for i in range(4)]
    )
    near = lax.ppermute(
        jnp.concatenate([cols(me ^ 1), far[frames:]], axis=0), axis, [(i, i ^ 1) for i in range(4)]
    )
    return jnp.concatenate([cols(me), far[:frames], near], axis=0)


def on_device(
    inputs, layer_norm_gain, layer_norm_bias, w_in, dw_kernel, bn_gain, bn_bias, cotangent
):
    tok_rows = inputs.shape[0]
    features = inputs.shape[1]
    kernel_len = dw_kernel.shape[0]
    all_frames = tok_rows * lax.axis_size("seq") * lax.axis_size("fsdp")
    frames = inputs.astype(jnp.float32)
    row_mean = jnp.mean(frames, axis=-1, keepdims=True)
    centered_rows = frames - row_mean
    row_inverse_deviation = lax.rsqrt(
        jnp.mean(centered_rows * centered_rows, axis=-1, keepdims=True) + epsilon
    )
    standardized_input = centered_rows * row_inverse_deviation
    normalized_rows = (standardized_input * layer_norm_gain + layer_norm_bias).astype(jnp.bfloat16)
    full_weight = gather_rows(w_in, "fsdp")
    hidden = jnp.dot(normalized_rows, full_weight, preferred_element_type=jnp.float32)
    value_part = hidden[:, :features]
    gate_sig = jax.nn.sigmoid(hidden[:, features:])
    glu = (value_part * gate_sig).astype(jnp.bfloat16)
    past_rim = from_behind(glu[tok_rows - (kernel_len - 1) :], ("seq", "fsdp"), 1)
    padded_glu = jnp.concatenate([past_rim, glu], axis=0).astype(jnp.float32)
    conv_out = jnp.zeros((tok_rows, features), jnp.float32)
    for offset in range(kernel_len):
        conv_out = (
            conv_out
            + dw_kernel[offset]
            * padded_glu[kernel_len - 1 - offset : kernel_len - 1 - offset + tok_rows]
        )
    chan_mean, chan_var = mean_and_var(conv_out, ("seq", "fsdp"))
    conv_centred = conv_out - chan_mean
    bn_rstd = lax.rsqrt(chan_var + epsilon)
    chat = conv_centred * bn_rstd
    z_value = chat * bn_gain + bn_bias
    z_sig = jax.nn.sigmoid(z_value)
    output = (z_value * z_sig).astype(jnp.bfloat16)
    grad_z = cotangent.astype(jnp.float32) * z_sig * (1.0 + z_value * (1.0 - z_sig))
    grad_bn_bias, grad_bn_gain = tree_sum(
        (jnp.sum(grad_z, axis=0), jnp.sum(grad_z * chat, axis=0)), ("seq", "fsdp")
    )
    grad_conv = (
        bn_gain * bn_rstd * (grad_z - grad_bn_bias / all_frames - chat * grad_bn_gain / all_frames)
    )
    future_rim = from_behind(grad_conv[: kernel_len - 1], ("seq", "fsdp"), -1)
    padded_grad = jnp.concatenate([grad_conv, future_rim], axis=0)
    grad_glu = jnp.zeros((tok_rows, features), jnp.float32)
    for offset in range(kernel_len):
        grad_glu = grad_glu + dw_kernel[offset] * padded_grad[offset : offset + tok_rows]
    grad_value = grad_glu * gate_sig
    grad_gate = grad_glu * value_part * gate_sig * (1.0 - gate_sig)
    grad_hidden = jnp.concatenate([grad_value, grad_gate], axis=1).astype(jnp.bfloat16)
    late_grad_conv, late_glu, grad_hidden = lax.optimization_barrier(
        (grad_conv, padded_glu, grad_hidden)
    )
    kernel_rows = []
    for offset in range(kernel_len):
        kernel_rows.append(
            jnp.sum(
                late_grad_conv
                * late_glu[kernel_len - 1 - offset : kernel_len - 1 - offset + tok_rows],
                axis=0,
            )
        )
    kernel_portion = jnp.stack(kernel_rows, axis=0)
    normalized_gradient = lax.dot_general(
        grad_hidden, full_weight, (((1,), (1,)), ((), ())), preferred_element_type=jnp.float32
    )
    rescaled_rows = normalized_gradient * layer_norm_gain
    input_gradient = row_inverse_deviation * (
        rescaled_rows
        - jnp.mean(rescaled_rows, axis=-1, keepdims=True)
        - standardized_input * jnp.mean(rescaled_rows * standardized_input, axis=-1, keepdims=True)
    )
    local_sums = (
        kernel_portion,
        jnp.sum(normalized_gradient * standardized_input, axis=0),
        jnp.sum(normalized_gradient, axis=0),
    )
    feature_rows = w_in.shape[0]
    group_rows = gather_own_columns(normalized_rows, "fsdp", feature_rows)
    contract = (((0,), (0,)), ((), ()))
    if lax.axis_size("fsdp") == 4:
        far = lax.ppermute(grad_hidden, "fsdp", [(i, i ^ 2) for i in range(4)])
        near = lax.ppermute(grad_hidden, "fsdp", [(i, i ^ 1) for i in range(4)])
        far, input_gradient, local_sums = lax.optimization_barrier(
            (far, input_gradient, local_sums)
        )
        near_far = lax.ppermute(far, "fsdp", [(i, i ^ 1) for i in range(4)])
        pieces = (grad_hidden, far, near, near_far)
        row_share = None
        for slot, piece in enumerate(pieces):
            term = lax.dot_general(
                group_rows[slot * tok_rows : (slot + 1) * tok_rows],
                piece,
                contract,
                preferred_element_type=jnp.float32,
            )
            row_share = term if row_share is None else row_share + term
    else:
        group_grad = lax.all_gather(grad_hidden, "fsdp", axis=0, tiled=True)
        row_share = lax.dot_general(
            group_rows, group_grad, contract, preferred_element_type=jnp.float32
        )
    reduced = lax.psum_scatter(row_share, "seq", scatter_dimension=0, tiled=True)
    grad_w_in = lax.all_gather(
        reduced.astype(jnp.bfloat16), "seq", axis=0, tiled=True
    ).astype(jnp.float32)
    grad_kernel, layer_norm_gain_gradient, grad_ln_bias = tree_sum(local_sums, ("seq", "fsdp"))
    return (
        output,
        input_gradient.astype(jnp.bfloat16),
        grad_w_in,
        grad_kernel,
        grad_bn_gain,
        grad_bn_bias,
        layer_norm_gain_gradient,
        grad_ln_bias,
    )


def solution(mesh):
    placed = (
        P(("seq", "fsdp"), None),
        P(),
        P(),
        P("fsdp", None),
        P(),
        P(),
        P(),
        P(("seq", "fsdp"), None),
    )
    return jax.shard_map(
        on_device,
        mesh=mesh,
        in_specs=placed,
        out_specs=(
            P(("seq", "fsdp"), None),
            P(("seq", "fsdp"), None),
            P("fsdp", None),
            P(),
            P(),
            P(),
            P(),
            P(),
        ),
        check_vma=False,
    )
```

```python
import jax
import jax.numpy as jnp
from jax import lax
from jax.sharding import PartitionSpec as P

epsilon = 1e-05


def from_behind(block, axis, distance):
    devices = range(lax.axis_size(axis))
    route = [(i - distance, i) for i in devices if i - distance in devices]
    return lax.ppermute(block, axis, route)


def tree_sum(tree, axis):
    count = lax.axis_size(axis)
    if count & (count - 1):
        return lax.psum(tree, axis)
    leaves, treedef = jax.tree.flatten(tree)
    width = leaves[0].shape[-1]
    packed = jnp.concatenate([leaf.reshape(-1, width) for leaf in leaves], axis=0)
    stride = 1
    while stride < count:
        route = [(i, i ^ stride) for i in range(count)]
        packed = packed + lax.ppermute(packed, axis, route)
        stride *= 2
    out, start = [], 0
    for leaf in leaves:
        rows = leaf.size // width
        out.append(packed[start : start + rows].reshape(leaf.shape))
        start += rows
    return jax.tree.unflatten(treedef, out)


def mean_and_var(block, axis):
    count = lax.axis_size(axis)
    frames = block.shape[0]
    if count & (count - 1):
        total = count * frames
        mean = lax.psum(jnp.sum(block, axis=0), axis) / total
        centred = block - mean
        return mean, lax.psum(jnp.sum(centred * centred, axis=0), axis) / total
    mean = jnp.mean(block, axis=0)
    centred = block - mean
    spread = jnp.sum(centred * centred, axis=0)
    stats = jnp.stack([mean, spread])
    rows, stride = frames, 1
    while stride < count:
        other = lax.ppermute(stats, axis, [(i, i ^ stride) for i in range(count)])
        delta = stats[0] - other[0]
        stats = jnp.stack(
            [
                (stats[0] + other[0]) * 0.5,
                (stats[1] + other[1]) + (0.5 * rows) * (delta * delta),
            ]
        )
        rows, stride = rows * 2, stride * 2
    return stats[0], stats[1] / rows


def group_shards(block, axis):
    far = lax.ppermute(block, axis, [(i, i ^ 2) for i in range(4)])
    near = lax.ppermute(block, axis, [(i, i ^ 1) for i in range(4)])
    near_far = lax.ppermute(far, axis, [(i, i ^ 1) for i in range(4)])
    return [block, far, near, near_far]


def gather_rows(block, axis):
    count = lax.axis_size(axis)
    if count != 4:
        return lax.all_gather(block, axis, axis=0, tiled=True)
    rows = block.shape[0]
    me = lax.axis_index(axis)
    shards = group_shards(block, axis)
    whole = jnp.zeros((count * rows,) + block.shape[1:], block.dtype)
    for shard, owner in zip(shards, (me, me ^ 2, me ^ 1, me ^ 3)):
        whole = lax.dynamic_update_slice_in_dim(whole, shard, owner * rows, axis=0)
    return whole


def gather_own_columns(rows_block, axis, width):
    me = lax.axis_index(axis)
    frames = rows_block.shape[0]

    def cols(owner):
        return lax.dynamic_slice_in_dim(rows_block, owner * width, width, axis=1)

    if lax.axis_size(axis) != 4:
        return lax.dynamic_slice_in_dim(
            lax.all_gather(rows_block, axis, axis=0, tiled=True), me * width, width, axis=1
        )
    far = lax.ppermute(
        jnp.concatenate([cols(me ^ 2), cols(me ^ 3)], axis=0), axis, [(i, i ^ 2) for i in range(4)]
    )
    near = lax.ppermute(
        jnp.concatenate([cols(me ^ 1), far[frames:]], axis=0), axis, [(i, i ^ 1) for i in range(4)]
    )
    return jnp.concatenate([cols(me), far[:frames], near], axis=0)


def on_device(
    inputs, layer_norm_gain, layer_norm_bias, w_in, dw_kernel, bn_gain, bn_bias, cotangent
):
    tok_rows = inputs.shape[0]
    features = inputs.shape[1]
    kernel_len = dw_kernel.shape[0]
    all_frames = tok_rows * lax.axis_size("seq") * lax.axis_size("fsdp")
    frames = inputs.astype(jnp.float32)
    row_mean = jnp.mean(frames, axis=-1, keepdims=True)
    centered_rows = frames - row_mean
    row_inverse_deviation = lax.rsqrt(
        jnp.mean(centered_rows * centered_rows, axis=-1, keepdims=True) + epsilon
    )
    standardized_input = centered_rows * row_inverse_deviation
    normalized_rows = (standardized_input * layer_norm_gain + layer_norm_bias).astype(jnp.bfloat16)
    full_weight = gather_rows(w_in, "fsdp")
    hidden = jnp.dot(normalized_rows, full_weight, preferred_element_type=jnp.float32)
    value_part = hidden[:, :features]
    gate_sig = jax.nn.sigmoid(hidden[:, features:])
    glu = (value_part * gate_sig).astype(jnp.bfloat16)
    past_rim = from_behind(glu[tok_rows - (kernel_len - 1) :], ("seq", "fsdp"), 1)
    padded_glu = jnp.concatenate([past_rim, glu], axis=0).astype(jnp.float32)
    conv_out = jnp.zeros((tok_rows, features), jnp.float32)
    for offset in range(kernel_len):
        conv_out = (
            conv_out
            + dw_kernel[offset]
            * padded_glu[kernel_len - 1 - offset : kernel_len - 1 - offset + tok_rows]
        )
    chan_mean, chan_var = mean_and_var(conv_out, ("seq", "fsdp"))
    conv_centred = conv_out - chan_mean
    bn_rstd = lax.rsqrt(chan_var + epsilon)
    chat = conv_centred * bn_rstd
    z_value = chat * bn_gain + bn_bias
    z_sig = jax.nn.sigmoid(z_value)
    output = (z_value * z_sig).astype(jnp.bfloat16)
    grad_z = cotangent.astype(jnp.float32) * z_sig * (1.0 + z_value * (1.0 - z_sig))
    grad_bn_bias, grad_bn_gain = tree_sum(
        (jnp.sum(grad_z, axis=0), jnp.sum(grad_z * chat, axis=0)), ("seq", "fsdp")
    )
    grad_conv = (
        bn_gain * bn_rstd * (grad_z - grad_bn_bias / all_frames - chat * grad_bn_gain / all_frames)
    )
    future_rim = from_behind(grad_conv[: kernel_len - 1], ("seq", "fsdp"), -1)
    padded_grad = jnp.concatenate([grad_conv, future_rim], axis=0)
    grad_glu = jnp.zeros((tok_rows, features), jnp.float32)
    for offset in range(kernel_len):
        grad_glu = grad_glu + dw_kernel[offset] * padded_grad[offset : offset + tok_rows]
    grad_value = grad_glu * gate_sig
    grad_gate = grad_glu * value_part * gate_sig * (1.0 - gate_sig)
    grad_hidden = jnp.concatenate([grad_value, grad_gate], axis=1).astype(jnp.bfloat16)
    late_grad_conv, late_glu, grad_hidden = lax.optimization_barrier(
        (grad_conv, padded_glu, grad_hidden)
    )
    kernel_rows = []
    for offset in range(kernel_len):
        kernel_rows.append(
            jnp.sum(
                late_grad_conv
                * late_glu[kernel_len - 1 - offset : kernel_len - 1 - offset + tok_rows],
                axis=0,
            )
        )
    kernel_portion = jnp.stack(kernel_rows, axis=0)
    normalized_gradient = lax.dot_general(
        grad_hidden, full_weight, (((1,), (1,)), ((), ())), preferred_element_type=jnp.float32
    )
    rescaled_rows = normalized_gradient * layer_norm_gain
    input_gradient = row_inverse_deviation * (
        rescaled_rows
        - jnp.mean(rescaled_rows, axis=-1, keepdims=True)
        - standardized_input * jnp.mean(rescaled_rows * standardized_input, axis=-1, keepdims=True)
    )
    local_sums = (
        kernel_portion,
        jnp.sum(normalized_gradient * standardized_input, axis=0),
        jnp.sum(normalized_gradient, axis=0),
    )
    feature_rows = w_in.shape[0]
    group_rows = gather_own_columns(normalized_rows, "fsdp", feature_rows)
    contract = (((0,), (0,)), ((), ()))
    if lax.axis_size("fsdp") == 4:
        far = lax.ppermute(grad_hidden, "fsdp", [(i, i ^ 2) for i in range(4)])
        near = lax.ppermute(grad_hidden, "fsdp", [(i, i ^ 1) for i in range(4)])
        far, input_gradient, local_sums = lax.optimization_barrier(
            (far, input_gradient, local_sums)
        )
        near_far = lax.ppermute(far, "fsdp", [(i, i ^ 1) for i in range(4)])
        pieces = (grad_hidden, far, near, near_far)
        row_share = None
        for slot, piece in enumerate(pieces):
            term = lax.dot_general(
                group_rows[slot * tok_rows : (slot + 1) * tok_rows],
                piece,
                contract,
                preferred_element_type=jnp.float32,
            )
            row_share = term if row_share is None else row_share + term
    else:
        group_grad = lax.all_gather(grad_hidden, "fsdp", axis=0, tiled=True)
        row_share = lax.dot_general(
            group_rows, group_grad, contract, preferred_element_type=jnp.float32
        )
    reduced = lax.psum_scatter(row_share, "seq", scatter_dimension=0, tiled=True)
    parameter_grads = tree_sum(local_sums, ("seq", "fsdp"))
    reduced, parameter_grads = lax.optimization_barrier((reduced, parameter_grads))
    grad_kernel, layer_norm_gain_gradient, grad_ln_bias = parameter_grads
    grad_w_in = lax.all_gather(
        reduced.astype(jnp.bfloat16), "seq", axis=0, tiled=True
    ).astype(jnp.float32)
    return (
        output,
        input_gradient.astype(jnp.bfloat16),
        grad_w_in,
        grad_kernel,
        grad_bn_gain,
        grad_bn_bias,
        layer_norm_gain_gradient,
        grad_ln_bias,
    )


def solution(mesh):
    placed = (
        P(("seq", "fsdp"), None),
        P(),
        P(),
        P("fsdp", None),
        P(),
        P(),
        P(),
        P(("seq", "fsdp"), None),
    )
    return jax.shard_map(
        on_device,
        mesh=mesh,
        in_specs=placed,
        out_specs=(
            P(("seq", "fsdp"), None),
            P(("seq", "fsdp"), None),
            P("fsdp", None),
            P(),
            P(),
            P(),
            P(),
            P(),
        ),
        check_vma=False,
    )
```

```python
import jax
import jax.numpy as jnp
from jax import lax
from jax.sharding import PartitionSpec as P

epsilon = 1e-05


def from_behind(block, axis, distance):
    devices = range(lax.axis_size(axis))
    route = [(i - distance, i) for i in devices if i - distance in devices]
    return lax.ppermute(block, axis, route)


def tree_sum(tree, axis):
    count = lax.axis_size(axis)
    if count & (count - 1):
        return lax.psum(tree, axis)
    leaves, treedef = jax.tree.flatten(tree)
    width = leaves[0].shape[-1]
    packed = jnp.concatenate([leaf.reshape(-1, width) for leaf in leaves], axis=0)
    stride = 1
    while stride < count:
        route = [(i, i ^ stride) for i in range(count)]
        packed = packed + lax.ppermute(packed, axis, route)
        stride *= 2
    out, start = [], 0
    for leaf in leaves:
        rows = leaf.size // width
        out.append(packed[start : start + rows].reshape(leaf.shape))
        start += rows
    return jax.tree.unflatten(treedef, out)


def mean_and_var(block, axis):
    count = lax.axis_size(axis)
    frames = block.shape[0]
    if count & (count - 1):
        total = count * frames
        mean = lax.psum(jnp.sum(block, axis=0), axis) / total
        centred = block - mean
        return mean, lax.psum(jnp.sum(centred * centred, axis=0), axis) / total
    mean = jnp.mean(block, axis=0)
    centred = block - mean
    spread = jnp.sum(centred * centred, axis=0)
    stats = jnp.stack([mean, spread])
    rows, stride = frames, 1
    while stride < count:
        other = lax.ppermute(stats, axis, [(i, i ^ stride) for i in range(count)])
        delta = stats[0] - other[0]
        stats = jnp.stack(
            [
                (stats[0] + other[0]) * 0.5,
                (stats[1] + other[1]) + (0.5 * rows) * (delta * delta),
            ]
        )
        rows, stride = rows * 2, stride * 2
    return stats[0], stats[1] / rows


def group_shards(block, axis):
    far = lax.ppermute(block, axis, [(i, i ^ 2) for i in range(4)])
    near = lax.ppermute(block, axis, [(i, i ^ 1) for i in range(4)])
    near_far = lax.ppermute(far, axis, [(i, i ^ 1) for i in range(4)])
    return [block, far, near, near_far]


def gather_rows(block, axis):
    count = lax.axis_size(axis)
    if count != 4:
        return lax.all_gather(block, axis, axis=0, tiled=True)
    rows = block.shape[0]
    me = lax.axis_index(axis)
    shards = group_shards(block, axis)
    whole = jnp.zeros((count * rows,) + block.shape[1:], block.dtype)
    for shard, owner in zip(shards, (me, me ^ 2, me ^ 1, me ^ 3)):
        whole = lax.dynamic_update_slice_in_dim(whole, shard, owner * rows, axis=0)
    return whole


def gather_own_columns(rows_block, axis, width):
    me = lax.axis_index(axis)
    frames = rows_block.shape[0]

    def cols(owner):
        return lax.dynamic_slice_in_dim(rows_block, owner * width, width, axis=1)

    if lax.axis_size(axis) != 4:
        return lax.dynamic_slice_in_dim(
            lax.all_gather(rows_block, axis, axis=0, tiled=True), me * width, width, axis=1
        )
    far = lax.ppermute(
        jnp.concatenate([cols(me ^ 2), cols(me ^ 3)], axis=0), axis, [(i, i ^ 2) for i in range(4)]
    )
    near = lax.ppermute(
        jnp.concatenate([cols(me ^ 1), far[frames:]], axis=0), axis, [(i, i ^ 1) for i in range(4)]
    )
    return jnp.concatenate([cols(me), far[:frames], near], axis=0)


def on_device(
    inputs, layer_norm_gain, layer_norm_bias, w_in, dw_kernel, bn_gain, bn_bias, cotangent
):
    tok_rows = inputs.shape[0]
    features = inputs.shape[1]
    kernel_len = dw_kernel.shape[0]
    all_frames = tok_rows * lax.axis_size("seq") * lax.axis_size("fsdp")
    frames = inputs.astype(jnp.float32)
    row_mean = jnp.mean(frames, axis=-1, keepdims=True)
    centered_rows = frames - row_mean
    row_inverse_deviation = lax.rsqrt(
        jnp.mean(centered_rows * centered_rows, axis=-1, keepdims=True) + epsilon
    )
    standardized_input = centered_rows * row_inverse_deviation
    normalized_rows = (standardized_input * layer_norm_gain + layer_norm_bias).astype(jnp.bfloat16)
    full_weight = gather_rows(w_in, "fsdp")
    hidden = jnp.dot(normalized_rows, full_weight, preferred_element_type=jnp.float32)
    value_part = hidden[:, :features]
    gate_sig = jax.nn.sigmoid(hidden[:, features:])
    glu = (value_part * gate_sig).astype(jnp.bfloat16)
    past_rim = from_behind(glu[tok_rows - (kernel_len - 1) :], ("seq", "fsdp"), 1)
    padded_glu = jnp.concatenate([past_rim, glu], axis=0).astype(jnp.float32)
    conv_out = jnp.zeros((tok_rows, features), jnp.float32)
    for offset in range(kernel_len):
        conv_out = (
            conv_out
            + dw_kernel[offset]
            * padded_glu[kernel_len - 1 - offset : kernel_len - 1 - offset + tok_rows]
        )
    chan_mean, chan_var = mean_and_var(conv_out, ("seq", "fsdp"))
    conv_centred = conv_out - chan_mean
    bn_rstd = lax.rsqrt(chan_var + epsilon)
    chat = conv_centred * bn_rstd
    z_value = chat * bn_gain + bn_bias
    z_sig = jax.nn.sigmoid(z_value)
    output = (z_value * z_sig).astype(jnp.bfloat16)
    grad_z = cotangent.astype(jnp.float32) * z_sig * (1.0 + z_value * (1.0 - z_sig))
    late_rows, _ = lax.optimization_barrier((normalized_rows, hidden))
    group_rows = gather_own_columns(late_rows, "fsdp", w_in.shape[0])
    group_rows, bn_partials = lax.optimization_barrier(
        (group_rows, (jnp.sum(grad_z, axis=0), jnp.sum(grad_z * chat, axis=0)))
    )
    grad_bn_bias, grad_bn_gain = tree_sum(bn_partials, ("seq", "fsdp"))
    grad_conv = (
        bn_gain * bn_rstd * (grad_z - grad_bn_bias / all_frames - chat * grad_bn_gain / all_frames)
    )
    future_rim = from_behind(grad_conv[: kernel_len - 1], ("seq", "fsdp"), -1)
    padded_grad = jnp.concatenate([grad_conv, future_rim], axis=0)
    grad_glu = jnp.zeros((tok_rows, features), jnp.float32)
    for offset in range(kernel_len):
        grad_glu = grad_glu + dw_kernel[offset] * padded_grad[offset : offset + tok_rows]
    grad_value = grad_glu * gate_sig
    grad_gate = grad_glu * value_part * gate_sig * (1.0 - gate_sig)
    grad_hidden = jnp.concatenate([grad_value, grad_gate], axis=1).astype(jnp.bfloat16)
    late_grad_conv, late_glu, grad_hidden = lax.optimization_barrier(
        (grad_conv, padded_glu, grad_hidden)
    )
    kernel_rows = []
    for offset in range(kernel_len):
        kernel_rows.append(
            jnp.sum(
                late_grad_conv
                * late_glu[kernel_len - 1 - offset : kernel_len - 1 - offset + tok_rows],
                axis=0,
            )
        )
    kernel_portion = jnp.stack(kernel_rows, axis=0)
    normalized_gradient = lax.dot_general(
        grad_hidden, full_weight, (((1,), (1,)), ((), ())), preferred_element_type=jnp.float32
    )
    rescaled_rows = normalized_gradient * layer_norm_gain
    input_gradient = row_inverse_deviation * (
        rescaled_rows
        - jnp.mean(rescaled_rows, axis=-1, keepdims=True)
        - standardized_input * jnp.mean(rescaled_rows * standardized_input, axis=-1, keepdims=True)
    )
    local_sums = (
        kernel_portion,
        jnp.sum(normalized_gradient * standardized_input, axis=0),
        jnp.sum(normalized_gradient, axis=0),
    )
    feature_rows = w_in.shape[0]
    contract = (((0,), (0,)), ((), ()))
    if lax.axis_size("fsdp") == 4:
        far = lax.ppermute(grad_hidden, "fsdp", [(i, i ^ 2) for i in range(4)])
        near = lax.ppermute(grad_hidden, "fsdp", [(i, i ^ 1) for i in range(4)])
        far, input_gradient, local_sums = lax.optimization_barrier(
            (far, input_gradient, local_sums)
        )
        near_far = lax.ppermute(far, "fsdp", [(i, i ^ 1) for i in range(4)])
        pieces = (grad_hidden, far, near, near_far)
        row_share = None
        for slot, piece in enumerate(pieces):
            term = lax.dot_general(
                group_rows[slot * tok_rows : (slot + 1) * tok_rows],
                piece,
                contract,
                preferred_element_type=jnp.float32,
            )
            row_share = term if row_share is None else row_share + term
    else:
        group_grad = lax.all_gather(grad_hidden, "fsdp", axis=0, tiled=True)
        row_share = lax.dot_general(
            group_rows, group_grad, contract, preferred_element_type=jnp.float32
        )
    reduced = lax.psum_scatter(row_share, "seq", scatter_dimension=0, tiled=True)
    grad_w_in = lax.all_gather(
        reduced.astype(jnp.bfloat16), "seq", axis=0, tiled=True
    ).astype(jnp.float32)
    grad_kernel, layer_norm_gain_gradient, grad_ln_bias = tree_sum(local_sums, ("seq", "fsdp"))
    return (
        output,
        input_gradient.astype(jnp.bfloat16),
        grad_w_in,
        grad_kernel,
        grad_bn_gain,
        grad_bn_bias,
        layer_norm_gain_gradient,
        grad_ln_bias,
    )


def solution(mesh):
    placed = (
        P(("seq", "fsdp"), None),
        P(),
        P(),
        P("fsdp", None),
        P(),
        P(),
        P(),
        P(("seq", "fsdp"), None),
    )
    return jax.shard_map(
        on_device,
        mesh=mesh,
        in_specs=placed,
        out_specs=(
            P(("seq", "fsdp"), None),
            P(("seq", "fsdp"), None),
            P("fsdp", None),
            P(),
            P(),
            P(),
            P(),
            P(),
        ),
        check_vma=False,
    )
```
